512 devices in a mesh: teach: 64 (over z, y), seq: 8 (over x, core).
Axes of the slice: x: 4, y: 8, z: 8, core: 2. Of those that a mesh axis runs over, the one named last changes fastest.
Arguments:
- teacher_in: bfloat16 [2048, 4, 5120], P('teach', None, 'seq'), may hold values from -6 to 6
- teacher_proj: bfloat16 [64, 5120, 512], P('teach', 'seq'), may hold values from -0.078125 to 0.078125
- family: int32 [2048, 4, 1], replicated, may hold values from 0 to 7; in each aligned block of 128 rows (0 to 127, 128 to 255, ..., all dimensions but the last counted through in order) at most 32 rows name the same one
- x_in: bfloat16 [2048, 4, 64, 64], P('seq', None, 'teach'), may hold values from -6 to 6
- b_in: bfloat16 [2048, 4, 64, 128], P('seq', None, 'teach'), may hold values from -1.796875 to 1.796875
- c_in: bfloat16 [2048, 4, 64, 128], P('seq', None, 'teach'), may hold values from -1.796875 to 1.796875
- step_size: float32 [2048, 4, 64], P('seq', None, 'teach'), may hold values from 0.02 to 0.1
- doc_start: int32 [2048, 4], P('seq'), may hold values from 0 to 1, as said below
- a_rate: float32 [64], P('teach'), may hold values from 0.001953125 to 1
- skip_gain: float32 [64], P('teach'), may hold values from 0.5 to 1.5
Outputs:
- grad_x: bfloat16 [2048, 4, 64, 64], P('seq', None, 'teach')
- grad_b: bfloat16 [2048, 4, 64, 128], P('seq', None, 'teach')
- grad_c: bfloat16 [2048, 4, 64, 128], P('seq', None, 'teach')
The draws below stay inside these ranges and needn't reach their ends.
Inputs may be any that keep to these rules, and one draw needn't show every extreme that they name: In each source block of 128 rows no family appears more than 32 times, and in some source block some family appears exactly 32 times. `doc_start`: in each sequence exactly two ones: at position 0 and at one position from 512 up to 1536.
All inputs are finite; a program needn't handle non-finite values.
Results may differ from the reference program's by a relative error of at most 0.011.
Values may be sent and summed in bfloat16 or wider, within the bound.
No kernel may reach another device: no remote copies, remote signals or barrier semaphores. Data moves between devices by JAX's collectives and lax.ppermute only.
A program may use at most 64 MiB of HBM per device.

```python
import math
import jax
import jax.numpy as jnp
import numpy as np
from jax import lax

TD = 5120
P_SIZE = 64
N = 128
FAM = 8
BATCH = 4
SEQ_LEN = 2048
ROWS = 128
HEADS = 64
CAP = 32
COPIES = 8
GROUP_COLS = 8
N_TEACH = 64


def draw_doc_start(key, part):
    second = jax.random.randint(jax.random.fold_in(key, 17), (BATCH,), SEQ_LEN // 4, 3 * SEQ_LEN // 4 + 1)
    places = jnp.arange(SEQ_LEN, dtype=jnp.int32)[:, None]
    return ((places == 0) | (places == second[None, :])).astype(jnp.int32)


def steps_of(rng, shape, cuts, least, largest):
    def one(axis_at, parts):
        draws = jax.random.uniform(jax.random.fold_in(jax.random.fold_in(rng, 6), axis_at), (parts,), jnp.float32, least / len(cuts), largest / len(cuts))
        return jnp.repeat(jnp.exp(draws), shape[axis_at] // parts).reshape((-1,) + (1,) * (len(shape) - axis_at - 1))

    factor_of = one(*cuts[0])
    for cut in cuts[1:]:
        factor_of = factor_of * one(*cut)
    return factor_of


def deal_out(rng, own, number, rows, count, top, bound, skew):
    ranking = jax.random.permutation(rng, count)
    crowded, ordinary = shares(count, rows * top, bound, skew, True), shares(count, rows * top, bound, skew, False)
    places = jnp.arange(count)

    def named(sizes, rotation):
        used = int((sizes > 0).sum())
        fixed = max(1, used // 4)
        shifted = fixed + (places - fixed + rotation * (used - fixed)) % max(1, count - fixed)
        return jnp.zeros((count,), jnp.int32).at[ranking[jnp.where(places < fixed, places, shifted)]].set(jnp.asarray(sizes, jnp.int32))

    sizes = jnp.where(number % 4 == 0, named(crowded, number // 4), named(ordinary, number - number // 4 - 1))
    mixed = jax.random.permutation(jax.random.fold_in(own, 3), count)
    source_of, taker = mixed[0:count // 2 * 2:2], mixed[1:count // 2 * 2:2]
    margin = jnp.minimum(sizes[source_of] - 1, bound - sizes[taker]) // 2
    margin = jnp.where((source_of == ranking[0]) | (taker == ranking[0]) | (sizes[taker] == 0), 0, jnp.maximum(margin, 0))
    shifted = jax.random.randint(jax.random.fold_in(own, 4), (count // 2,), 0, 1 << 20) % (margin + 1)
    sizes = sizes.at[source_of].add(-shifted).at[taker].add(shifted)
    members = jnp.searchsorted(jnp.cumsum(sizes), jnp.arange(rows * top), side="right").astype(jnp.int32)
    grid = members.reshape(top, rows).T
    grid = grid[jax.random.permutation(jax.random.fold_in(own, 1), rows)]
    rotation = jax.random.randint(jax.random.fold_in(own, 2), (rows, 1), 0, top)
    return jnp.take_along_axis(grid, (jnp.arange(top)[None, :] + rotation) % top, axis=1)


def shares(number_of, total, most, slope, full):
    loads = [(1 << 20) // math.isqrt(grade ** slope) + 1 for grade in range(1, number_of + 1)]
    largest = most if full else min(most, max(-(-total // number_of), total * loads[0] // sum(loads)))
    least = 1 if total - largest >= number_of - 1 else 0
    holding, rest = [largest] + [least] * (number_of - 1), total - largest - least * (number_of - 1)
    while rest > 0:
        free = [i for i in range(1, number_of) if holding[i] < largest] or [i for i in range(1, number_of) if holding[i] < most]
        mass, remaining = sum([loads[i] for i in free]), rest
        for i in free:
            more = min(most - holding[i], max(1, remaining * loads[i] // mass), rest)
            holding[i] = holding[i] + more
            rest = rest - more
    return np.array(holding)


def noise(stream_key, dims, scale, bound, shards=(), kind=jnp.bfloat16):
    values = scale * jax.random.normal(stream_key, dims, jnp.float32)
    if shards:
        values = values * steps_of(stream_key, dims, shards, -0.22, 0.18)
    return jnp.clip(values, -bound, bound).astype(kind)


def setup_inputs(seed: int = 0) -> dict:
    streams_of = jax.random.split(jax.random.key(seed), 11)
    teacher_in = noise(streams_of[0], (SEQ_LEN, BATCH, TD), 1.0, 6.0, ((0, 64), (2, 8)))
    teacher_proj = noise(streams_of[1], (N_TEACH, TD, HEADS * GROUP_COLS), TD ** -0.5, 0.078125, ((0, 64), (1, 8)))
    family_keys = jax.random.split(jax.random.fold_in(streams_of[2], 1), SEQ_LEN * BATCH // ROWS)
    family_turns = jax.random.permutation(jax.random.fold_in(streams_of[2], 3), SEQ_LEN * BATCH // ROWS)
    family = jax.vmap(lambda own, number: deal_out(jax.random.fold_in(streams_of[2], 2), own, number, ROWS, FAM, 1, CAP, 2))(family_keys, family_turns).reshape((SEQ_LEN, BATCH, 1))
    x_in = noise(streams_of[3], (SEQ_LEN, BATCH, HEADS, P_SIZE), 1.0, 6.0, ((0, 8), (2, 64)))
    b_in = noise(streams_of[4], (SEQ_LEN, BATCH, HEADS, N), 0.3, 1.796875, ((0, 8), (2, 64)))
    c_in = noise(streams_of[5], (SEQ_LEN, BATCH, HEADS, N), 0.3, 1.796875, ((0, 8), (2, 64)))
    step_size = jnp.clip(jnp.exp(math.log(0.1) - 1.609438 * jax.random.uniform(streams_of[6], (SEQ_LEN, BATCH, HEADS), jnp.float32) ** steps_of(streams_of[6], (SEQ_LEN, BATCH, HEADS), ((0, 8), (2, 64)), -0.2, 0.2)), 0.02, 0.1)
    doc_start = draw_doc_start(jax.random.fold_in(streams_of[10], 71), 0)
    a_rate = jnp.clip(jnp.exp(math.log(1.0) - 6.2383246 * jax.random.uniform(streams_of[8], (HEADS,), jnp.float32) ** steps_of(streams_of[8], (HEADS,), ((0, 64),), -0.2, 0.2)), 0.001953125, 1.0)
    skip_gain = jnp.clip(0.5 + 1.0 * jax.random.uniform(streams_of[9], (HEADS,), jnp.float32) ** steps_of(streams_of[9], (HEADS,), ((0, 64),), -0.2, 0.2), 0.5, 1.5)
    return {"teacher_in": teacher_in, "teacher_proj": teacher_proj, "family": family, "x_in": x_in, "b_in": b_in, "c_in": c_in, "step_size": step_size, "doc_start": doc_start, "a_rate": a_rate, "skip_gain": skip_gain}


EPS = 1e-06
HIGH = lax.Precision.HIGHEST

def family_slots(fam_block):
    onehot = (fam_block[..., None] == jnp.arange(FAM, dtype=jnp.int32)[None, None, :]).astype(jnp.int32)
    before = jnp.cumsum(onehot, axis=1) - onehot
    return lax.optimization_barrier(jnp.sum(before * onehot, axis=2)).astype(jnp.int32)

def decay_matrix(log_sums, counts):
    places = jnp.arange(log_sums.shape[0])
    keep_mask = (places[:, None] >= places[None, :]) & (counts[:, None] == counts[None, :])
    gaps = log_sums.T[:, :, None] - log_sums.T[:, None, :]
    return jnp.where(keep_mask[None], jnp.exp(jnp.where(keep_mask[None], gaps, 0.0)), 0.0)

def block_terms(x_in, b_in, c_in, step_size, doc_start, a_rate):
    log_sums = jnp.cumsum(-step_size * a_rate[None, :], axis=0)
    counts = jnp.cumsum(doc_start)
    to_end = jnp.exp(log_sums[-1][None, :] - log_sums) * (counts == counts[-1]).astype(jnp.float32)[:, None]
    from_start = jnp.exp(log_sums) * (counts == 0).astype(jnp.float32)[:, None]
    through = jnp.exp(log_sums[-1]) * (counts[-1] == 0).astype(jnp.float32)
    inputs = step_size[:, :, None] * x_in.astype(jnp.float32)
    decay_mat = decay_matrix(log_sums, counts)
    scores = jnp.einsum('ihn,jhn->hij', c_in.astype(jnp.float32), b_in.astype(jnp.float32), precision=HIGH)
    return (to_end, from_start, through, inputs, decay_mat, decay_mat * scores)

def forward_block(terms, x_in, c_in, skip_gain, state_in):
    to_end, from_start, through, inputs, decay_mat, mixing = terms
    c_full = c_in.astype(jnp.float32)
    output = jnp.einsum('hij,jhp->ihp', mixing, inputs, precision=HIGH)
    output = output + from_start[:, :, None] * jnp.einsum('ihn,hpn->ihp', c_full, state_in, precision=HIGH)
    return output + skip_gain[None, :, None] * x_in.astype(jnp.float32)

def backward_block(terms, b_in, c_in, step_size, skip_gain, residual, state_in, adjoint_in):
    to_end, from_start, through, inputs, decay_mat, mixing = terms
    b_full = b_in.astype(jnp.float32)
    c_full = c_in.astype(jnp.float32)
    grad_u = jnp.einsum('hij,ihp->jhp', mixing, residual, precision=HIGH)
    grad_u = grad_u + to_end[:, :, None] * jnp.einsum('jhn,hnp->jhp', b_full, adjoint_in, precision=HIGH)
    grad_x = step_size[:, :, None] * grad_u + skip_gain[None, :, None] * residual
    pair = decay_mat * jnp.einsum('ihp,jhp->hij', residual, inputs, precision=HIGH)
    grad_b = jnp.einsum('hij,ihn->jhn', pair, c_full, precision=HIGH)
    grad_b = grad_b + to_end[:, :, None] * jnp.einsum('jhp,hnp->jhn', inputs, adjoint_in, precision=HIGH)
    grad_c = jnp.einsum('hij,jhn->ihn', pair, b_full, precision=HIGH)
    grad_c = grad_c + from_start[:, :, None] * jnp.einsum('ihp,hpn->ihn', residual, state_in, precision=HIGH)
    return (grad_x, grad_b, grad_c)

def student_sequence(x_in, b_in, c_in, step_size, doc_start, target, a_rate, skip_gain):
    span = min(512, SEQ_LEN)
    count_blocks = SEQ_LEN // span
    state = jnp.zeros((HEADS, P_SIZE, N), jnp.float32)
    saved = []
    for block_id in range(count_blocks):
        lo = block_id * span
        terms = block_terms(x_in[lo:lo + span], b_in[lo:lo + span], c_in[lo:lo + span], step_size[lo:lo + span], doc_start[lo:lo + span], a_rate)
        output = forward_block(terms, x_in[lo:lo + span], c_in[lo:lo + span], skip_gain, state)
        residual = output - target[lo:lo + span].astype(jnp.float32)
        saved.append((terms, state, residual))
        local_state = jnp.einsum('jh,jhp,jhn->hpn', terms[0], terms[3], b_in[lo:lo + span].astype(jnp.float32), precision=HIGH)
        state = terms[2][:, None, None] * state + local_state
    adjoint = jnp.zeros((HEADS, N, P_SIZE), jnp.float32)
    pieces_x, pieces_b, pieces_c = ([], [], [])
    for block_id in reversed(range(count_blocks)):
        lo = block_id * span
        terms, state_in, residual = saved[block_id]
        grad_x, grad_b, grad_c = backward_block(terms, b_in[lo:lo + span], c_in[lo:lo + span], step_size[lo:lo + span], skip_gain, residual, state_in, adjoint)
        pieces_x.insert(0, grad_x)
        pieces_b.insert(0, grad_b)
        pieces_c.insert(0, grad_c)
        local_adjoint = jnp.einsum('ih,ihn,ihp->hnp', terms[1], c_in[lo:lo + span].astype(jnp.float32), residual, precision=HIGH)
        adjoint = terms[2][:, None, None] * adjoint + local_adjoint
    grad_x = jnp.concatenate(pieces_x, axis=0).astype(jnp.bfloat16)
    grad_b = jnp.concatenate(pieces_b, axis=0).astype(jnp.bfloat16)
    grad_c = jnp.concatenate(pieces_c, axis=0).astype(jnp.bfloat16)
    return (grad_x, grad_b, grad_c)

def reference(teacher_in, teacher_proj, family, x_in, b_in, c_in, step_size, doc_start, a_rate, skip_gain):
    total_rows = SEQ_LEN * BATCH
    rows_all = teacher_in.reshape(total_rows, TD)
    fam_all = family.reshape(total_rows).astype(jnp.int32)
    fam_block = fam_all.reshape(N_TEACH, ROWS)
    slot_ids = family_slots(fam_block)
    sources = jnp.arange(N_TEACH, dtype=jnp.int32)[:, None]
    dest_rows = ((fam_block * N_TEACH + sources) * CAP + slot_ids).reshape(total_rows).astype(jnp.int32)
    total_slots = FAM * N_TEACH * CAP
    slot_source = jnp.full((total_slots,), total_rows, jnp.int32).at[dest_rows].set(jnp.arange(total_rows, dtype=jnp.int32))
    sq_sums = lax.optimization_barrier(jnp.sum(jnp.square(rows_all.astype(jnp.float32)), axis=1))
    row_scale = lax.rsqrt(sq_sums / TD + EPS)
    per_owner = teacher_proj.reshape(COPIES, FAM, TD, HEADS, GROUP_COLS)

    def family_step(f_index, target_flat):
        family_proj = lax.dynamic_index_in_dim(per_owner, f_index, axis=1, keepdims=False)
        family_proj = family_proj.transpose(1, 2, 0, 3).reshape(TD, HEADS * P_SIZE)
        source_ids = lax.dynamic_slice_in_dim(slot_source, f_index * (N_TEACH * CAP), N_TEACH * CAP)
        safe_ids = jnp.minimum(source_ids, total_rows - 1)
        slot_block = rows_all[safe_ids]
        product = jnp.dot(slot_block, family_proj, preferred_element_type=jnp.float32)
        values = (product * row_scale[safe_ids][:, None]).astype(jnp.bfloat16)
        return target_flat.at[source_ids].set(values, mode='drop')
    target_flat = lax.fori_loop(0, FAM, family_step, jnp.zeros((total_rows, HEADS * P_SIZE), jnp.bfloat16))
    target = target_flat.reshape(SEQ_LEN, BATCH, HEADS, P_SIZE)

    def one_sequence(items):
        x_one, b_one, c_one, step_one, doc_one, target_one = items
        return student_sequence(x_one, b_one, c_one, step_one, doc_one, target_one, a_rate, skip_gain)
    items = (x_in.transpose(1, 0, 2, 3), b_in.transpose(1, 0, 2, 3), c_in.transpose(1, 0, 2, 3), step_size.transpose(1, 0, 2), doc_start.T, target.transpose(1, 0, 2, 3))
    grad_x, grad_b, grad_c = lax.map(one_sequence, items)
    return (grad_x.transpose(1, 0, 2, 3), grad_b.transpose(1, 0, 2, 3), grad_c.transpose(1, 0, 2, 3))
```

```python
import jax
import jax.numpy as jnp
from jax import lax
from jax.sharding import Mesh
from jax.sharding import PartitionSpec as P

TD = 5120
P_SIZE = 64
FAM = 8
CAP = 32


EPS = 1e-06
HIGH = lax.Precision.HIGHEST
QUADRATIC = lax.Precision.HIGH
TEACH = ("tz", "ty")


def family_slots(fam_block):
    onehot = (fam_block[..., None] == jnp.arange(FAM, dtype=jnp.int32)[None, None, :]).astype(
        jnp.int32
    )
    before = jnp.cumsum(onehot, axis=1) - onehot
    return jnp.sum(before * onehot, axis=2)


def decay_matrix(log_sums, counts):
    places = jnp.arange(log_sums.shape[0])
    lower = places[:, None] >= places[None, :]
    same_doc = counts.T[:, :, None] == counts.T[:, None, :]
    keep_mask = (lower[None] & same_doc)[:, None]
    sums = log_sums.transpose(1, 2, 0)
    gaps = sums[:, :, :, None] - sums[:, :, None, :]
    return jnp.where(keep_mask, jnp.exp(jnp.where(keep_mask, gaps, 0.0)), 0.0)


def chain_weights(through_all, place, backward):
    count = through_all.shape[0]
    blocks = jnp.arange(count)
    s2 = blocks[:, None]
    s3 = blocks[None, :]
    if backward:
        used = (s3 > place) & (s3 < s2)
        live = blocks > place
    else:
        used = (s3 > s2) & (s3 < place)
        live = blocks < place
    factors = jnp.where(used[:, :, None, None], through_all[None], 1.0)
    weights = jnp.prod(factors, axis=1)
    return jnp.where(live[:, None, None], weights, 0.0)


def carried(local, through, axis, backward):
    place = lax.axis_index(axis)
    through_all = lax.all_gather(through, axis)
    local_all = lax.all_gather(local, axis)
    weights = chain_weights(through_all, place, backward)
    return jnp.sum(weights[:, :, :, None, None] * local_all, axis=0)


def per_device(
    teacher_in, teacher_proj, family, x_in, b_in, c_in, step_size, doc_start, a_rate, skip_gain
):
    n_z = lax.axis_size("tz")
    n_y = lax.axis_size("ty")
    seq_n = lax.axis_size("seq")
    teach_n = n_z * n_y
    heads_all = teach_n * x_in.shape[2]
    block_pos = teacher_in.shape[0]
    batch_n = teacher_in.shape[1]
    feat_width = teacher_in.shape[2]
    block_rows = block_pos * batch_n
    source = lax.axis_index("tz") * n_y + lax.axis_index("ty")
    fam_all = family.reshape(family.shape[0] * family.shape[1])

    own_rows = teacher_in.reshape(block_rows, feat_width)
    own_fam = lax.dynamic_slice_in_dim(fam_all, source * block_rows, block_rows)
    slot_ids = family_slots(own_fam.reshape(1, block_rows))[0]
    dest_cols = own_fam * CAP + slot_ids
    select = (dest_cols[:, None] == jnp.arange(FAM * CAP, dtype=jnp.int32)[None, :]).astype(
        jnp.bfloat16
    )
    packed = jnp.dot(select.T, own_rows, preferred_element_type=jnp.float32).astype(jnp.bfloat16)
    packed = packed.reshape(FAM, CAP, feat_width)
    by_family = lax.all_to_all(packed, "ty", split_axis=0, concat_axis=0, tiled=True)
    received = lax.all_gather(by_family, "tz")
    slots_all = n_z * n_y * CAP
    received = received.reshape(slots_all, feat_width)
    weights = teacher_proj[0]
    partial_value = jnp.dot(received, weights, preferred_element_type=jnp.float32)
    sq_sums = jnp.sum(jnp.square(received.astype(jnp.float32)), axis=1)
    partial_value = partial_value.reshape(n_z, n_y * CAP, heads_all, -1)
    sq_sums = sq_sums.reshape(n_z, n_y * CAP)
    summed = lax.psum_scatter(partial_value, "seq", scatter_dimension=0, tiled=True)[0]
    totals = lax.psum_scatter(sq_sums, "seq", scatter_dimension=0, tiled=True)[0]
    row_scale = lax.rsqrt(totals / TD + EPS)
    scaled = (summed * row_scale[:, None, None]).astype(jnp.bfloat16)
    cols = scaled.shape[-1]
    outgoing = scaled.transpose(1, 0, 2)
    arrived = lax.all_to_all(outgoing, TEACH, split_axis=0, concat_axis=0, tiled=True)
    arrived = arrived.reshape(n_z, n_y, n_y * CAP, cols)
    table = arrived.transpose(1, 2, 0, 3).reshape(n_y * n_y * CAP, n_z * cols)

    shard_rows = n_y * block_rows
    shard_fam = lax.dynamic_slice_in_dim(
        fam_all, lax.axis_index("seq") * shard_rows, shard_rows
    ).reshape(n_y, block_rows)
    shard_slots = family_slots(shard_fam)
    sources = jnp.arange(n_y, dtype=jnp.int32)[:, None]
    row_index = ((shard_fam * n_y + sources) * CAP + shard_slots).reshape(shard_rows)
    picked = jnp.take(table, row_index, axis=0)
    target = picked.reshape(n_y * block_pos, batch_n, 1, P_SIZE)

    x_full = x_in.astype(jnp.float32)
    b_full = b_in.astype(jnp.float32)
    c_full = c_in.astype(jnp.float32)
    log_sums = jnp.cumsum(-step_size * a_rate[None, None, :], axis=0)
    counts = jnp.cumsum(doc_start, axis=0)
    same_end = (counts == counts[-1][None, :]).astype(jnp.float32)
    to_end = jnp.exp(log_sums[-1][None] - log_sums) * same_end[:, :, None]
    from_start = jnp.exp(log_sums) * (counts == 0).astype(jnp.float32)[:, :, None]
    through = jnp.exp(log_sums[-1]) * (counts[-1] == 0).astype(jnp.float32)[:, None]
    inputs = step_size[..., None] * x_full
    local_state = jnp.einsum("jbh,jbhp,jbhn->bhpn", to_end, inputs, b_full, precision=HIGH)
    state_in = carried(local_state, through, "seq", False)
    decay_mat = decay_matrix(log_sums, counts)
    scores = jnp.einsum("ibhn,jbhn->bhij", c_in, b_in, preferred_element_type=jnp.float32)
    mixing = decay_mat * scores
    output = jnp.einsum("bhij,jbhp->ibhp", mixing, inputs, precision=QUADRATIC)
    output = output + from_start[..., None] * jnp.einsum(
        "ibhn,bhpn->ibhp", c_full, state_in, precision=HIGH
    )
    output = output + skip_gain[None, None, :, None] * x_full
    residual = output - target.astype(jnp.float32)
    local_adjoint = jnp.einsum("ibh,ibhn,ibhp->bhnp", from_start, c_full, residual, precision=HIGH)
    adjoint_in = carried(local_adjoint, through, "seq", True)
    grad_u = jnp.einsum("bhij,ibhp->jbhp", mixing, residual, precision=QUADRATIC)
    grad_u = grad_u + to_end[..., None] * jnp.einsum(
        "jbhn,bhnp->jbhp", b_full, adjoint_in, precision=HIGH
    )
    grad_x = step_size[..., None] * grad_u + skip_gain[None, None, :, None] * residual
    pair = decay_mat * jnp.einsum("ibhp,jbhp->bhij", residual, inputs, precision=QUADRATIC)
    grad_b = jnp.einsum("bhij,ibhn->jbhn", pair, c_full, precision=QUADRATIC)
    grad_b = grad_b + to_end[..., None] * jnp.einsum(
        "jbhp,bhnp->jbhn", inputs, adjoint_in, precision=HIGH
    )
    grad_c = jnp.einsum("bhij,jbhn->ibhn", pair, b_full, precision=QUADRATIC)
    grad_c = grad_c + from_start[..., None] * jnp.einsum(
        "ibhp,bhpn->ibhn", residual, state_in, precision=HIGH
    )
    return (grad_x.astype(jnp.bfloat16), grad_b.astype(jnp.bfloat16), grad_c.astype(jnp.bfloat16))


def solution(mesh):
    teach_n, seq_n = mesh.devices.shape
    n_y = FAM
    n_z = teach_n // n_y
    assert n_z == seq_n
    split = Mesh(mesh.devices.reshape(n_z, n_y, seq_n), ("tz", "ty", "seq"))
    placed = (
        P(TEACH, None, "seq"),
        P(TEACH, "seq", None),
        P(),
        P("seq", None, TEACH, None),
        P("seq", None, TEACH, None),
        P("seq", None, TEACH, None),
        P("seq", None, TEACH),
        P("seq", None),
        P(TEACH),
        P(TEACH),
    )
    return jax.shard_map(
        per_device,
        mesh=split,
        in_specs=placed,
        out_specs=(
            P("seq", None, TEACH, None),
            P("seq", None, TEACH, None),
            P("seq", None, TEACH, None),
        ),
        check_vma=False,
    )
```

```python
import jax
import jax.numpy as jnp
from jax import lax
from jax.sharding import Mesh
from jax.sharding import PartitionSpec as P

TD = 5120
P_SIZE = 64
FAM = 8
CAP = 32


EPS = 1e-06
HIGH = lax.Precision.HIGHEST
QUADRATIC = lax.Precision.HIGH
TEACH = ("tz", "ty")


def family_slots(fam_block):
    onehot = (fam_block[..., None] == jnp.arange(FAM, dtype=jnp.int32)[None, None, :]).astype(
        jnp.int32
    )
    before = jnp.cumsum(onehot, axis=1) - onehot
    return jnp.sum(before * onehot, axis=2)


def decay_matrix(log_sums, counts):
    places = jnp.arange(log_sums.shape[0])
    lower = places[:, None] >= places[None, :]
    same_doc = counts.T[:, :, None] == counts.T[:, None, :]
    keep_mask = (lower[None] & same_doc)[:, None]
    sums = log_sums.transpose(1, 2, 0)
    gaps = sums[:, :, :, None] - sums[:, :, None, :]
    return jnp.where(keep_mask, jnp.exp(jnp.where(keep_mask, gaps, 0.0)), 0.0)


def carried(local, through, axis, backward):
    count = lax.axis_size(axis)
    total = jnp.zeros_like(local)
    weight = jnp.ones_like(through)
    for hop in range(1, count):
        if backward:
            pairs = [(src, src - hop) for src in range(hop, count)]
        else:
            pairs = [(src, src + hop) for src in range(count - hop)]
        got_local, got_through = lax.ppermute((local, through), axis, pairs)
        total = total + weight[:, :, None, None] * got_local
        weight = weight * got_through
    return total


def per_device(
    teacher_in, teacher_proj, family, x_in, b_in, c_in, step_size, doc_start, a_rate, skip_gain
):
    n_z = lax.axis_size("tz")
    n_y = lax.axis_size("ty")
    seq_n = lax.axis_size("seq")
    teach_n = n_z * n_y
    heads_all = teach_n * x_in.shape[2]
    block_pos = teacher_in.shape[0]
    batch_n = teacher_in.shape[1]
    feat_width = teacher_in.shape[2]
    block_rows = block_pos * batch_n
    source = lax.axis_index("tz") * n_y + lax.axis_index("ty")
    fam_all = family.reshape(family.shape[0] * family.shape[1])

    own_rows = teacher_in.reshape(block_rows, feat_width)
    own_fam = lax.dynamic_slice_in_dim(fam_all, source * block_rows, block_rows)
    slot_ids = family_slots(own_fam.reshape(1, block_rows))[0]
    dest_cols = own_fam * CAP + slot_ids
    select = (dest_cols[:, None] == jnp.arange(FAM * CAP, dtype=jnp.int32)[None, :]).astype(
        jnp.bfloat16
    )
    packed = jnp.dot(select.T, own_rows, preferred_element_type=jnp.float32).astype(jnp.bfloat16)
    packed = packed.reshape(FAM, CAP, feat_width)
    by_family = lax.all_to_all(packed, "ty", split_axis=0, concat_axis=0, tiled=True)
    received = lax.all_gather(by_family, "tz")
    slots_all = n_z * n_y * CAP
    received = received.reshape(slots_all, feat_width)
    weights = teacher_proj[0]
    partial_value = jnp.dot(received, weights, preferred_element_type=jnp.float32)
    sq_sums = jnp.sum(jnp.square(received.astype(jnp.float32)), axis=1)
    partial_value = partial_value.reshape(n_z, n_y * CAP, heads_all, -1)
    sq_sums = sq_sums.reshape(n_z, n_y * CAP)
    summed = lax.psum_scatter(
        partial_value.astype(jnp.bfloat16), "seq", scatter_dimension=0, tiled=True
    )[0].astype(jnp.float32)
    totals = lax.psum_scatter(sq_sums, "seq", scatter_dimension=0, tiled=True)[0]
    row_scale = lax.rsqrt(totals / TD + EPS)
    scaled = (summed * row_scale[:, None, None]).astype(jnp.bfloat16)
    cols = scaled.shape[-1]
    outgoing = scaled.transpose(1, 0, 2)
    arrived = lax.all_to_all(outgoing, TEACH, split_axis=0, concat_axis=0, tiled=True)
    arrived = arrived.reshape(n_z, n_y, n_y * CAP, cols)
    table = arrived.transpose(1, 2, 0, 3).reshape(n_y * n_y * CAP, n_z * cols)

    shard_rows = n_y * block_rows
    shard_fam = lax.dynamic_slice_in_dim(
        fam_all, lax.axis_index("seq") * shard_rows, shard_rows
    ).reshape(n_y, block_rows)
    shard_slots = family_slots(shard_fam)
    sources = jnp.arange(n_y, dtype=jnp.int32)[:, None]
    row_index = ((shard_fam * n_y + sources) * CAP + shard_slots).reshape(shard_rows)
    picked = jnp.take(table, row_index, axis=0)
    target = picked.reshape(n_y * block_pos, batch_n, 1, P_SIZE)

    x_full = x_in.astype(jnp.float32)
    b_full = b_in.astype(jnp.float32)
    c_full = c_in.astype(jnp.float32)
    log_sums = jnp.cumsum(-step_size * a_rate[None, None, :], axis=0)
    counts = jnp.cumsum(doc_start, axis=0)
    same_end = (counts == counts[-1][None, :]).astype(jnp.float32)
    to_end = jnp.exp(log_sums[-1][None] - log_sums) * same_end[:, :, None]
    from_start = jnp.exp(log_sums) * (counts == 0).astype(jnp.float32)[:, :, None]
    through = jnp.exp(log_sums[-1]) * (counts[-1] == 0).astype(jnp.float32)[:, None]
    inputs = step_size[..., None] * x_full
    local_state = jnp.einsum("jbh,jbhp,jbhn->bhpn", to_end, inputs, b_full, precision=HIGH)
    state_in = carried(local_state, through, "seq", False)
    decay_mat = decay_matrix(log_sums, counts)
    scores = jnp.einsum("ibhn,jbhn->bhij", c_in, b_in, preferred_element_type=jnp.float32)
    mixing = decay_mat * scores
    output = jnp.einsum("bhij,jbhp->ibhp", mixing, inputs, precision=QUADRATIC)
    output = output + from_start[..., None] * jnp.einsum(
        "ibhn,bhpn->ibhp", c_full, state_in, precision=HIGH
    )
    output = output + skip_gain[None, None, :, None] * x_full
    residual = output - target.astype(jnp.float32)
    local_adjoint = jnp.einsum("ibh,ibhn,ibhp->bhnp", from_start, c_full, residual, precision=HIGH)
    adjoint_in = carried(local_adjoint, through, "seq", True)
    grad_u = jnp.einsum("bhij,ibhp->jbhp", mixing, residual, precision=QUADRATIC)
    grad_u = grad_u + to_end[..., None] * jnp.einsum(
        "jbhn,bhnp->jbhp", b_full, adjoint_in, precision=HIGH
    )
    grad_x = step_size[..., None] * grad_u + skip_gain[None, None, :, None] * residual
    pair = decay_mat * jnp.einsum("ibhp,jbhp->bhij", residual, inputs, precision=QUADRATIC)
    grad_b = jnp.einsum("bhij,ibhn->jbhn", pair, c_full, precision=QUADRATIC)
    grad_b = grad_b + to_end[..., None] * jnp.einsum(
        "jbhp,bhnp->jbhn", inputs, adjoint_in, precision=HIGH
    )
    grad_c = jnp.einsum("bhij,jbhn->ibhn", pair, b_full, precision=QUADRATIC)
    grad_c = grad_c + from_start[..., None] * jnp.einsum(
        "ibhp,bhpn->ibhn", residual, state_in, precision=HIGH
    )
    return (grad_x.astype(jnp.bfloat16), grad_b.astype(jnp.bfloat16), grad_c.astype(jnp.bfloat16))


def solution(mesh):
    teach_n, seq_n = mesh.devices.shape
    n_y = FAM
    n_z = teach_n // n_y
    assert n_z == seq_n
    split = Mesh(mesh.devices.reshape(n_z, n_y, seq_n), ("tz", "ty", "seq"))
    placed = (
        P(TEACH, None, "seq"),
        P(TEACH, "seq", None),
        P(),
        P("seq", None, TEACH, None),
        P("seq", None, TEACH, None),
        P("seq", None, TEACH, None),
        P("seq", None, TEACH),
        P("seq", None),
        P(TEACH),
        P(TEACH),
    )
    return jax.shard_map(
        per_device,
        mesh=split,
        in_specs=placed,
        out_specs=(
            P("seq", None, TEACH, None),
            P("seq", None, TEACH, None),
            P("seq", None, TEACH, None),
        ),
        check_vma=False,
    )
```

```python
import jax
import jax.numpy as jnp
from jax import lax
from jax.sharding import Mesh
from jax.sharding import PartitionSpec as P

TD = 5120
P_SIZE = 64
FAM = 8
CAP = 32


EPS = 1e-06
HIGH = lax.Precision.HIGHEST
QUADRATIC = lax.Precision.HIGH
TEACH = ("tz", "ty")


def family_slots(fam_block):
    onehot = (fam_block[..., None] == jnp.arange(FAM, dtype=jnp.int32)[None, None, :]).astype(
        jnp.int32
    )
    before = jnp.cumsum(onehot, axis=1) - onehot
    return jnp.sum(before * onehot, axis=2)


def decay_matrix(log_sums, counts):
    places = jnp.arange(log_sums.shape[0])
    lower = places[:, None] >= places[None, :]
    same_doc = counts.T[:, :, None] == counts.T[:, None, :]
    keep_mask = (lower[None] & same_doc)[:, None]
    sums = log_sums.transpose(1, 2, 0)
    gaps = sums[:, :, :, None] - sums[:, :, None, :]
    return jnp.where(keep_mask, jnp.exp(jnp.where(keep_mask, gaps, 0.0)), 0.0)


def chain_weights(through_all, place, backward):
    count = through_all.shape[0]
    blocks = jnp.arange(count)
    s2 = blocks[:, None]
    s3 = blocks[None, :]
    if backward:
        used = (s3 > place) & (s3 < s2)
        live = blocks > place
    else:
        used = (s3 > s2) & (s3 < place)
        live = blocks < place
    factors = jnp.where(used[:, :, None, None], through_all[None], 1.0)
    weights = jnp.prod(factors, axis=1)
    return jnp.where(live[:, None, None], weights, 0.0)


def combine(weights, local_all):
    return jnp.sum(weights[:, :, :, None, None] * local_all.astype(jnp.float32), axis=0)


def per_device(
    teacher_in, teacher_proj, family, x_in, b_in, c_in, step_size, doc_start, a_rate, skip_gain
):
    n_z = lax.axis_size("tz")
    n_y = lax.axis_size("ty")
    seq_n = lax.axis_size("seq")
    teach_n = n_z * n_y
    heads_all = teach_n * x_in.shape[2]
    block_pos = teacher_in.shape[0]
    batch_n = teacher_in.shape[1]
    feat_width = teacher_in.shape[2]
    block_rows = block_pos * batch_n
    source = lax.axis_index("tz") * n_y + lax.axis_index("ty")
    fam_all = family.reshape(family.shape[0] * family.shape[1])

    own_rows = teacher_in.reshape(block_rows, feat_width)
    own_fam = lax.dynamic_slice_in_dim(fam_all, source * block_rows, block_rows)
    slot_ids = family_slots(own_fam.reshape(1, block_rows))[0]
    dest_cols = own_fam * CAP + slot_ids
    select = (dest_cols[:, None] == jnp.arange(FAM * CAP, dtype=jnp.int32)[None, :]).astype(
        jnp.bfloat16
    )
    packed = jnp.dot(select.T, own_rows, preferred_element_type=jnp.float32).astype(jnp.bfloat16)
    packed = packed.reshape(FAM, CAP, feat_width)
    by_family = lax.all_to_all(packed, "ty", split_axis=0, concat_axis=0, tiled=True)
    received = lax.all_gather(by_family, "tz")
    slots_all = n_z * n_y * CAP
    received = received.reshape(slots_all, feat_width)
    weights = teacher_proj[0]
    partial_value = jnp.dot(received, weights, preferred_element_type=jnp.float32)
    sq_sums = jnp.sum(jnp.square(received.astype(jnp.float32)), axis=1)
    partial_value = partial_value.reshape(n_z, n_y * CAP, heads_all, -1)
    sq_sums = sq_sums.reshape(n_z, n_y * CAP)
    summed = lax.psum_scatter(partial_value, "seq", scatter_dimension=0, tiled=True)[0]
    totals = lax.psum_scatter(sq_sums, "seq", scatter_dimension=0, tiled=True)[0]
    row_scale = lax.rsqrt(totals / TD + EPS)
    scaled = (summed * row_scale[:, None, None]).astype(jnp.bfloat16)
    cols = scaled.shape[-1]
    outgoing = scaled.transpose(1, 0, 2)
    arrived = lax.all_to_all(outgoing, TEACH, split_axis=0, concat_axis=0, tiled=True)
    arrived = arrived.reshape(n_z, n_y, n_y * CAP, cols)
    table = arrived.transpose(1, 2, 0, 3).reshape(n_y * n_y * CAP, n_z * cols)

    shard_rows = n_y * block_rows
    shard_fam = lax.dynamic_slice_in_dim(
        fam_all, lax.axis_index("seq") * shard_rows, shard_rows
    ).reshape(n_y, block_rows)
    shard_slots = family_slots(shard_fam)
    sources = jnp.arange(n_y, dtype=jnp.int32)[:, None]
    row_index = ((shard_fam * n_y + sources) * CAP + shard_slots).reshape(shard_rows)
    picked = jnp.take(table, row_index, axis=0)
    target = picked.reshape(n_y * block_pos, batch_n, 1, P_SIZE)

    x_full = x_in.astype(jnp.float32)
    b_full = b_in.astype(jnp.float32)
    c_full = c_in.astype(jnp.float32)
    log_sums = jnp.cumsum(-step_size * a_rate[None, None, :], axis=0)
    counts = jnp.cumsum(doc_start, axis=0)
    same_end = (counts == counts[-1][None, :]).astype(jnp.float32)
    to_end = jnp.exp(log_sums[-1][None] - log_sums) * same_end[:, :, None]
    from_start = jnp.exp(log_sums) * (counts == 0).astype(jnp.float32)[:, :, None]
    through = jnp.exp(log_sums[-1]) * (counts[-1] == 0).astype(jnp.float32)[:, None]
    inputs = step_size[..., None] * x_full
    local_state = jnp.einsum("jbh,jbhp,jbhn->bhpn", to_end, inputs, b_full, precision=HIGH)
    place = lax.axis_index("seq")
    through_hi = through.astype(jnp.bfloat16)
    through_lo = (through - through_hi.astype(jnp.float32)).astype(jnp.bfloat16)
    edge = local_state.shape[-1]
    packed_state = jnp.concatenate(
        [
            local_state.astype(jnp.bfloat16),
            jnp.broadcast_to(through_hi[:, :, None, None], through.shape + (1, edge)),
            jnp.broadcast_to(through_lo[:, :, None, None], through.shape + (1, edge)),
        ],
        axis=2,
    )
    gathered = lax.all_gather(packed_state, "seq")
    rows = local_state.shape[2]
    through_all = gathered[:, :, :, rows, 0].astype(jnp.float32) + gathered[
        :, :, :, rows + 1, 0
    ].astype(jnp.float32)
    state_in = combine(chain_weights(through_all, place, False), gathered[:, :, :, :rows])
    decay_mat = decay_matrix(log_sums, counts)
    scores = jnp.einsum("ibhn,jbhn->bhij", c_in, b_in, preferred_element_type=jnp.float32)
    mixing = decay_mat * scores
    output = jnp.einsum("bhij,jbhp->ibhp", mixing, inputs, precision=QUADRATIC)
    output = output + from_start[..., None] * jnp.einsum(
        "ibhn,bhpn->ibhp", c_full, state_in, precision=HIGH
    )
    output = output + skip_gain[None, None, :, None] * x_full
    residual = output - target.astype(jnp.float32)
    local_adjoint = jnp.einsum("ibh,ibhn,ibhp->bhnp", from_start, c_full, residual, precision=HIGH)
    adjoint_all = lax.all_gather(local_adjoint.astype(jnp.bfloat16), "seq")
    adjoint_in = combine(chain_weights(through_all, place, True), adjoint_all)
    grad_u = jnp.einsum("bhij,ibhp->jbhp", mixing, residual, precision=QUADRATIC)
    grad_u = grad_u + to_end[..., None] * jnp.einsum(
        "jbhn,bhnp->jbhp", b_full, adjoint_in, precision=HIGH
    )
    grad_x = step_size[..., None] * grad_u + skip_gain[None, None, :, None] * residual
    pair = decay_mat * jnp.einsum("ibhp,jbhp->bhij", residual, inputs, precision=QUADRATIC)
    grad_b = jnp.einsum("bhij,ibhn->jbhn", pair, c_full, precision=QUADRATIC)
    grad_b = grad_b + to_end[..., None] * jnp.einsum(
        "jbhp,bhnp->jbhn", inputs, adjoint_in, precision=HIGH
    )
    grad_c = jnp.einsum("bhij,jbhn->ibhn", pair, b_full, precision=QUADRATIC)
    grad_c = grad_c + from_start[..., None] * jnp.einsum(
        "ibhp,bhpn->ibhn", residual, state_in, precision=HIGH
    )
    return (grad_x.astype(jnp.bfloat16), grad_b.astype(jnp.bfloat16), grad_c.astype(jnp.bfloat16))


def solution(mesh):
    teach_n, seq_n = mesh.devices.shape
    n_y = FAM
    n_z = teach_n // n_y
    assert n_z == seq_n
    split = Mesh(mesh.devices.reshape(n_z, n_y, seq_n), ("tz", "ty", "seq"))
    placed = (
        P(TEACH, None, "seq"),
        P(TEACH, "seq", None),
        P(),
        P("seq", None, TEACH, None),
        P("seq", None, TEACH, None),
        P("seq", None, TEACH, None),
        P("seq", None, TEACH),
        P("seq", None),
        P(TEACH),
        P(TEACH),
    )
    return jax.shard_map(
        per_device,
        mesh=split,
        in_specs=placed,
        out_specs=(
            P("seq", None, TEACH, None),
            P("seq", None, TEACH, None),
            P("seq", None, TEACH, None),
        ),
        check_vma=False,
    )
```

```python
import jax
import jax.numpy as jnp
from jax import lax
from jax.sharding import Mesh
from jax.sharding import PartitionSpec as P

TD = 5120
P_SIZE = 64
FAM = 8
CAP = 32


EPS = 1e-06
HIGH = lax.Precision.HIGHEST
QUADRATIC = lax.Precision.HIGH
TEACH = ("tz", "ty")


def family_slots(fam_block):
    onehot = (fam_block[..., None] == jnp.arange(FAM, dtype=jnp.int32)[None, None, :]).astype(
        jnp.int32
    )
    before = jnp.cumsum(onehot, axis=1) - onehot
    return jnp.sum(before * onehot, axis=2)


def decay_matrix(log_sums, counts):
    places = jnp.arange(log_sums.shape[0])
    lower = places[:, None] >= places[None, :]
    same_doc = counts.T[:, :, None] == counts.T[:, None, :]
    keep_mask = (lower[None] & same_doc)[:, None]
    sums = log_sums.transpose(1, 2, 0)
    gaps = sums[:, :, :, None] - sums[:, :, None, :]
    return jnp.where(keep_mask, jnp.exp(jnp.where(keep_mask, gaps, 0.0)), 0.0)


def chain_weights(through_all, place, backward):
    count = through_all.shape[0]
    blocks = jnp.arange(count)
    s2 = blocks[:, None]
    s3 = blocks[None, :]
    if backward:
        used = (s3 > place) & (s3 < s2)
        live = blocks > place
    else:
        used = (s3 > s2) & (s3 < place)
        live = blocks < place
    factors = jnp.where(used[:, :, None, None], through_all[None], 1.0)
    weights = jnp.prod(factors, axis=1)
    return jnp.where(live[:, None, None], weights, 0.0)


def combine(weights, local_all):
    return jnp.sum(weights[:, :, :, None, None] * local_all.astype(jnp.float32), axis=0)


def per_device(
    teacher_in, teacher_proj, family, x_in, b_in, c_in, step_size, doc_start, a_rate, skip_gain
):
    n_z = lax.axis_size("tz")
    n_y = lax.axis_size("ty")
    seq_n = lax.axis_size("seq")
    teach_n = n_z * n_y
    heads_all = teach_n * x_in.shape[2]
    block_pos = teacher_in.shape[0]
    batch_n = teacher_in.shape[1]
    feat_width = teacher_in.shape[2]
    block_rows = block_pos * batch_n
    source = lax.axis_index("tz") * n_y + lax.axis_index("ty")
    fam_all = family.reshape(family.shape[0] * family.shape[1])

    own_rows = teacher_in.reshape(block_rows, feat_width)
    own_fam = lax.dynamic_slice_in_dim(fam_all, source * block_rows, block_rows)
    slot_ids = family_slots(own_fam.reshape(1, block_rows))[0]
    dest_cols = own_fam * CAP + slot_ids
    select = (dest_cols[:, None] == jnp.arange(FAM * CAP, dtype=jnp.int32)[None, :]).astype(
        jnp.bfloat16
    )
    packed = jnp.dot(select.T, own_rows, preferred_element_type=jnp.float32).astype(jnp.bfloat16)
    packed = packed.reshape(FAM, CAP, feat_width)
    by_family = lax.all_to_all(packed, "ty", split_axis=0, concat_axis=0, tiled=True)
    received = lax.all_gather(by_family, "tz")
    x_full = x_in.astype(jnp.float32)
    b_full = b_in.astype(jnp.float32)
    c_full = c_in.astype(jnp.float32)
    log_sums = jnp.cumsum(-step_size * a_rate[None, None, :], axis=0)
    counts = jnp.cumsum(doc_start, axis=0)
    same_end = (counts == counts[-1][None, :]).astype(jnp.float32)
    to_end = jnp.exp(log_sums[-1][None] - log_sums) * same_end[:, :, None]
    from_start = jnp.exp(log_sums) * (counts == 0).astype(jnp.float32)[:, :, None]
    through = jnp.exp(log_sums[-1]) * (counts[-1] == 0).astype(jnp.float32)[:, None]
    inputs = step_size[..., None] * x_full
    local_state = jnp.einsum("jbh,jbhp,jbhn->bhpn", to_end, inputs, b_full, precision=HIGH)
    place = lax.axis_index("seq")
    through_hi = through.astype(jnp.bfloat16)
    through_lo = (through - through_hi.astype(jnp.float32)).astype(jnp.bfloat16)
    edge = local_state.shape[-1]
    packed_state = jnp.concatenate(
        [
            local_state.astype(jnp.bfloat16),
            jnp.broadcast_to(through_hi[:, :, None, None], through.shape + (1, edge)),
            jnp.broadcast_to(through_lo[:, :, None, None], through.shape + (1, edge)),
        ],
        axis=2,
    )
    gathered = lax.all_gather(packed_state, "seq")
    rows = local_state.shape[2]
    through_all = gathered[:, :, :, rows, 0].astype(jnp.float32) + gathered[
        :, :, :, rows + 1, 0
    ].astype(jnp.float32)
    slots_all = n_z * n_y * CAP
    received, gathered = lax.optimization_barrier((received, gathered))
    received = received.reshape(slots_all, feat_width)
    weights = teacher_proj[0]
    partial_value = jnp.dot(received, weights, preferred_element_type=jnp.float32)
    sq_sums = jnp.sum(jnp.square(received.astype(jnp.float32)), axis=1)
    width = partial_value.shape[-1]
    group = n_y * CAP
    partial_value = partial_value.reshape(n_z, group, width)
    sq_row = jnp.zeros((n_z, 1, width), jnp.float32).at[:, 0, :group].set(
        sq_sums.reshape(n_z, group)
    )
    summed = lax.psum_scatter(
        jnp.concatenate([partial_value, sq_row], axis=1), "seq", scatter_dimension=0, tiled=True
    )[0]
    row_scale = lax.rsqrt(summed[group, :group] / TD + EPS)
    scaled = (summed[:group] * row_scale[:, None]).astype(jnp.bfloat16)
    scaled = scaled.reshape(group, heads_all, -1)
    cols = scaled.shape[-1]
    outgoing = scaled.transpose(1, 0, 2)
    arrived = lax.all_to_all(outgoing, TEACH, split_axis=0, concat_axis=0, tiled=True)
    arrived = arrived.reshape(n_z, n_y, n_y * CAP, cols)
    table = arrived.transpose(1, 2, 0, 3).reshape(n_y * n_y * CAP, n_z * cols)

    shard_rows = n_y * block_rows
    shard_fam = lax.dynamic_slice_in_dim(
        fam_all, lax.axis_index("seq") * shard_rows, shard_rows
    ).reshape(n_y, block_rows)
    shard_slots = family_slots(shard_fam)
    sources = jnp.arange(n_y, dtype=jnp.int32)[:, None]
    row_index = ((shard_fam * n_y + sources) * CAP + shard_slots).reshape(shard_rows)
    picked = jnp.take(table, row_index, axis=0)
    target = picked.reshape(n_y * block_pos, batch_n, 1, P_SIZE)

    state_in = combine(chain_weights(through_all, place, False), gathered[:, :, :, :rows])
    decay_mat = decay_matrix(log_sums, counts)
    scores = jnp.einsum("ibhn,jbhn->bhij", c_in, b_in, preferred_element_type=jnp.float32)
    mixing = decay_mat * scores
    output = jnp.einsum("bhij,jbhp->ibhp", mixing, inputs, precision=QUADRATIC)
    output = output + from_start[..., None] * jnp.einsum(
        "ibhn,bhpn->ibhp", c_full, state_in, precision=HIGH
    )
    output = output + skip_gain[None, None, :, None] * x_full
    residual = output - target.astype(jnp.float32)
    local_adjoint = jnp.einsum("ibh,ibhn,ibhp->bhnp", from_start, c_full, residual, precision=HIGH)
    adjoint_all = lax.all_gather(local_adjoint.astype(jnp.bfloat16), "seq")
    adjoint_in = combine(chain_weights(through_all, place, True), adjoint_all)
    grad_u = jnp.einsum("bhij,ibhp->jbhp", mixing, residual, precision=QUADRATIC)
    grad_u = grad_u + to_end[..., None] * jnp.einsum(
        "jbhn,bhnp->jbhp", b_full, adjoint_in, precision=HIGH
    )
    grad_x = step_size[..., None] * grad_u + skip_gain[None, None, :, None] * residual
    pair = decay_mat * jnp.einsum("ibhp,jbhp->bhij", residual, inputs, precision=QUADRATIC)
    grad_b = jnp.einsum("bhij,ibhn->jbhn", pair, c_full, precision=QUADRATIC)
    grad_b = grad_b + to_end[..., None] * jnp.einsum(
        "jbhp,bhnp->jbhn", inputs, adjoint_in, precision=HIGH
    )
    grad_c = jnp.einsum("bhij,jbhn->ibhn", pair, b_full, precision=QUADRATIC)
    grad_c = grad_c + from_start[..., None] * jnp.einsum(
        "ibhp,bhpn->ibhn", residual, state_in, precision=HIGH
    )
    return (grad_x.astype(jnp.bfloat16), grad_b.astype(jnp.bfloat16), grad_c.astype(jnp.bfloat16))


def solution(mesh):
    teach_n, seq_n = mesh.devices.shape
    n_y = FAM
    n_z = teach_n // n_y
    assert n_z == seq_n
    split = Mesh(mesh.devices.reshape(n_z, n_y, seq_n), ("tz", "ty", "seq"))
    placed = (
        P(TEACH, None, "seq"),
        P(TEACH, "seq", None),
        P(),
        P("seq", None, TEACH, None),
        P("seq", None, TEACH, None),
        P("seq", None, TEACH, None),
        P("seq", None, TEACH),
        P("seq", None),
        P(TEACH),
        P(TEACH),
    )
    return jax.shard_map(
        per_device,
        mesh=split,
        in_specs=placed,
        out_specs=(
            P("seq", None, TEACH, None),
            P("seq", None, TEACH, None),
            P("seq", None, TEACH, None),
        ),
        check_vma=False,
    )
```

```python
import jax
import jax.numpy as jnp
from jax import lax
from jax.sharding import Mesh
from jax.sharding import PartitionSpec as P

TD = 5120
P_SIZE = 64
FAM = 8
CAP = 32


EPS = 1e-06
HIGH = lax.Precision.HIGHEST
QUADRATIC = lax.Precision.HIGH
TEACH = ("tz", "ty")


def family_slots(fam_block):
    onehot = (fam_block[..., None] == jnp.arange(FAM, dtype=jnp.int32)[None, None, :]).astype(
        jnp.int32
    )
    before = jnp.cumsum(onehot, axis=1) - onehot
    return jnp.sum(before * onehot, axis=2)


def decay_matrix(log_sums, counts):
    places = jnp.arange(log_sums.shape[0])
    lower = places[:, None] >= places[None, :]
    same_doc = counts.T[:, :, None] == counts.T[:, None, :]
    keep_mask = (lower[None] & same_doc)[:, None]
    sums = log_sums.transpose(1, 2, 0)
    gaps = sums[:, :, :, None] - sums[:, :, None, :]
    return jnp.where(keep_mask, jnp.exp(jnp.where(keep_mask, gaps, 0.0)), 0.0)


def chain_weights(through_all, place, backward):
    count = through_all.shape[0]
    blocks = jnp.arange(count)
    s2 = blocks[:, None]
    s3 = blocks[None, :]
    if backward:
        used = (s3 > place) & (s3 < s2)
        live = blocks > place
    else:
        used = (s3 > s2) & (s3 < place)
        live = blocks < place
    factors = jnp.where(used[:, :, None, None], through_all[None], 1.0)
    weights = jnp.prod(factors, axis=1)
    return jnp.where(live[:, None, None], weights, 0.0)


def combine(weights, local_all):
    return jnp.sum(weights[:, :, :, None, None] * local_all.astype(jnp.float32), axis=0)


def per_device(
    teacher_in, teacher_proj, family, x_in, b_in, c_in, step_size, doc_start, a_rate, skip_gain
):
    n_z = lax.axis_size("tz")
    n_y = lax.axis_size("ty")
    seq_n = lax.axis_size("seq")
    teach_n = n_z * n_y
    heads_all = teach_n * x_in.shape[2]
    block_pos = teacher_in.shape[0]
    batch_n = teacher_in.shape[1]
    feat_width = teacher_in.shape[2]
    block_rows = block_pos * batch_n
    source = lax.axis_index("tz") * n_y + lax.axis_index("ty")
    fam_all = family.reshape(family.shape[0] * family.shape[1])

    own_rows = teacher_in.reshape(block_rows, feat_width)
    own_fam = lax.dynamic_slice_in_dim(fam_all, source * block_rows, block_rows)
    slot_ids = family_slots(own_fam.reshape(1, block_rows))[0]
    dest_cols = own_fam * CAP + slot_ids
    select = (dest_cols[:, None] == jnp.arange(FAM * CAP, dtype=jnp.int32)[None, :]).astype(
        jnp.bfloat16
    )
    packed = jnp.dot(select.T, own_rows, preferred_element_type=jnp.float32).astype(jnp.bfloat16)
    packed = packed.reshape(FAM, CAP, feat_width)
    by_family = lax.all_to_all(packed, "ty", split_axis=0, concat_axis=0, tiled=True)
    received = lax.all_gather(by_family, "tz")
    x_full = x_in.astype(jnp.float32)
    b_full = b_in.astype(jnp.float32)
    c_full = c_in.astype(jnp.float32)
    log_sums = jnp.cumsum(-step_size * a_rate[None, None, :], axis=0)
    counts = jnp.cumsum(doc_start, axis=0)
    same_end = (counts == counts[-1][None, :]).astype(jnp.float32)
    to_end = jnp.exp(log_sums[-1][None] - log_sums) * same_end[:, :, None]
    from_start = jnp.exp(log_sums) * (counts == 0).astype(jnp.float32)[:, :, None]
    through = jnp.exp(log_sums[-1]) * (counts[-1] == 0).astype(jnp.float32)[:, None]
    inputs = step_size[..., None] * x_full
    local_state = jnp.einsum("jbh,jbhp,jbhn->bhpn", to_end, inputs, b_full, precision=HIGH)
    place = lax.axis_index("seq")
    through_hi = through.astype(jnp.bfloat16)
    through_lo = (through - through_hi.astype(jnp.float32)).astype(jnp.bfloat16)
    edge = local_state.shape[-1]
    packed_state = jnp.concatenate(
        [
            local_state.astype(jnp.bfloat16),
            jnp.broadcast_to(through_hi[:, :, None, None], through.shape + (1, edge)),
            jnp.broadcast_to(through_lo[:, :, None, None], through.shape + (1, edge)),
        ],
        axis=2,
    )
    gathered = lax.all_gather(packed_state, "seq")
    rows = local_state.shape[2]
    through_all = gathered[:, :, :, rows, 0].astype(jnp.float32) + gathered[
        :, :, :, rows + 1, 0
    ].astype(jnp.float32)
    slots_all = n_z * n_y * CAP
    received, gathered = lax.optimization_barrier((received, gathered))
    received = received.reshape(slots_all, feat_width)
    weights = teacher_proj[0]
    partial_value = jnp.dot(received, weights, preferred_element_type=jnp.float32)
    sq_sums = jnp.sum(jnp.square(received.astype(jnp.float32)), axis=1)
    width = partial_value.shape[-1]
    group = n_y * CAP
    partial_value = partial_value.reshape(n_z, group, width)
    sq_all = sq_sums.reshape(n_z, group)
    sq_hi = sq_all.astype(jnp.bfloat16)
    sq_lo = (sq_all - sq_hi.astype(jnp.float32)).astype(jnp.bfloat16)
    sq_row = jnp.zeros((n_z, 1, width), jnp.bfloat16)
    sq_row = sq_row.at[:, 0, :group].set(sq_hi).at[:, 0, group : 2 * group].set(sq_lo)
    outbound = jnp.concatenate([partial_value.astype(jnp.bfloat16), sq_row], axis=1)
    inbound = lax.all_to_all(outbound, "seq", split_axis=0, concat_axis=0, tiled=True)
    summed = jnp.sum(inbound.astype(jnp.float32), axis=0)
    sq_total = summed[group, :group] + summed[group, group : 2 * group]
    row_scale = lax.rsqrt(sq_total / TD + EPS)
    scaled = (summed[:group] * row_scale[:, None]).astype(jnp.bfloat16)
    scaled = scaled.reshape(group, heads_all, -1)
    cols = scaled.shape[-1]
    outgoing = scaled.transpose(1, 0, 2)
    arrived = lax.all_to_all(outgoing, TEACH, split_axis=0, concat_axis=0, tiled=True)
    arrived = arrived.reshape(n_z, n_y, n_y * CAP, cols)
    table = arrived.transpose(1, 2, 0, 3).reshape(n_y * n_y * CAP, n_z * cols)

    shard_rows = n_y * block_rows
    shard_fam = lax.dynamic_slice_in_dim(
        fam_all, lax.axis_index("seq") * shard_rows, shard_rows
    ).reshape(n_y, block_rows)
    shard_slots = family_slots(shard_fam)
    sources = jnp.arange(n_y, dtype=jnp.int32)[:, None]
    row_index = ((shard_fam * n_y + sources) * CAP + shard_slots).reshape(shard_rows)
    picked = jnp.take(table, row_index, axis=0)
    target = picked.reshape(n_y * block_pos, batch_n, 1, P_SIZE)

    state_in = combine(chain_weights(through_all, place, False), gathered[:, :, :, :rows])
    decay_mat = decay_matrix(log_sums, counts)
    scores = jnp.einsum("ibhn,jbhn->bhij", c_in, b_in, preferred_element_type=jnp.float32)
    mixing = decay_mat * scores
    output = jnp.einsum("bhij,jbhp->ibhp", mixing, inputs, precision=QUADRATIC)
    output = output + from_start[..., None] * jnp.einsum(
        "ibhn,bhpn->ibhp", c_full, state_in, precision=HIGH
    )
    output = output + skip_gain[None, None, :, None] * x_full
    residual = output - target.astype(jnp.float32)
    local_adjoint = jnp.einsum("ibh,ibhn,ibhp->bhnp", from_start, c_full, residual, precision=HIGH)
    adjoint_all = lax.all_gather(local_adjoint.astype(jnp.bfloat16), "seq")
    adjoint_in = combine(chain_weights(through_all, place, True), adjoint_all)
    grad_u = jnp.einsum("bhij,ibhp->jbhp", mixing, residual, precision=QUADRATIC)
    grad_u = grad_u + to_end[..., None] * jnp.einsum(
        "jbhn,bhnp->jbhp", b_full, adjoint_in, precision=HIGH
    )
    grad_x = step_size[..., None] * grad_u + skip_gain[None, None, :, None] * residual
    pair = decay_mat * jnp.einsum("ibhp,jbhp->bhij", residual, inputs, precision=QUADRATIC)
    grad_b = jnp.einsum("bhij,ibhn->jbhn", pair, c_full, precision=QUADRATIC)
    grad_b = grad_b + to_end[..., None] * jnp.einsum(
        "jbhp,bhnp->jbhn", inputs, adjoint_in, precision=HIGH
    )
    grad_c = jnp.einsum("bhij,jbhn->ibhn", pair, b_full, precision=QUADRATIC)
    grad_c = grad_c + from_start[..., None] * jnp.einsum(
        "ibhp,bhpn->ibhn", residual, state_in, precision=HIGH
    )
    return (grad_x.astype(jnp.bfloat16), grad_b.astype(jnp.bfloat16), grad_c.astype(jnp.bfloat16))


def solution(mesh):
    teach_n, seq_n = mesh.devices.shape
    n_y = FAM
    n_z = teach_n // n_y
    assert n_z == seq_n
    split = Mesh(mesh.devices.reshape(n_z, n_y, seq_n), ("tz", "ty", "seq"))
    placed = (
        P(TEACH, None, "seq"),
        P(TEACH, "seq", None),
        P(),
        P("seq", None, TEACH, None),
        P("seq", None, TEACH, None),
        P("seq", None, TEACH, None),
        P("seq", None, TEACH),
        P("seq", None),
        P(TEACH),
        P(TEACH),
    )
    return jax.shard_map(
        per_device,
        mesh=split,
        in_specs=placed,
        out_specs=(
            P("seq", None, TEACH, None),
            P("seq", None, TEACH, None),
            P("seq", None, TEACH, None),
        ),
        check_vma=False,
    )
```

```python
import jax
import jax.numpy as jnp
from jax import lax
from jax.sharding import Mesh
from jax.sharding import PartitionSpec as P

TD = 5120
P_SIZE = 64
FAM = 8
CAP = 32


EPS = 1e-06
HIGH = lax.Precision.HIGHEST
QUADRATIC = lax.Precision.HIGH
TEACH = ("tz", "ty")


def family_slots(fam_block):
    onehot = (fam_block[..., None] == jnp.arange(FAM, dtype=jnp.int32)[None, None, :]).astype(
        jnp.int32
    )
    before = jnp.cumsum(onehot, axis=1) - onehot
    return jnp.sum(before * onehot, axis=2)


def decay_matrix(log_sums, counts):
    places = jnp.arange(log_sums.shape[0])
    lower = places[:, None] >= places[None, :]
    same_doc = counts.T[:, :, None] == counts.T[:, None, :]
    keep_mask = (lower[None] & same_doc)[:, None]
    sums = log_sums.transpose(1, 2, 0)
    gaps = sums[:, :, :, None] - sums[:, :, None, :]
    return jnp.where(keep_mask, jnp.exp(jnp.where(keep_mask, gaps, 0.0)), 0.0)


def chain_weights(through_all, place, backward):
    count = through_all.shape[0]
    blocks = jnp.arange(count)
    s2 = blocks[:, None]
    s3 = blocks[None, :]
    if backward:
        used = (s3 > place) & (s3 < s2)
        live = blocks > place
    else:
        used = (s3 > s2) & (s3 < place)
        live = blocks < place
    factors = jnp.where(used[:, :, None, None], through_all[None], 1.0)
    weights = jnp.prod(factors, axis=1)
    return jnp.where(live[:, None, None], weights, 0.0)


def combine(weights, local_all):
    return jnp.sum(weights[:, :, :, None, None] * local_all.astype(jnp.float32), axis=0)


def per_device(
    teacher_in, teacher_proj, family, x_in, b_in, c_in, step_size, doc_start, a_rate, skip_gain
):
    n_z = lax.axis_size("tz")
    n_y = lax.axis_size("ty")
    seq_n = lax.axis_size("seq")
    teach_n = n_z * n_y
    heads_all = teach_n * x_in.shape[2]
    block_pos = teacher_in.shape[0]
    batch_n = teacher_in.shape[1]
    feat_width = teacher_in.shape[2]
    block_rows = block_pos * batch_n
    source = lax.axis_index("tz") * n_y + lax.axis_index("ty")
    fam_all = family.reshape(family.shape[0] * family.shape[1])

    own_rows = teacher_in.reshape(block_rows, feat_width)
    own_fam = lax.dynamic_slice_in_dim(fam_all, source * block_rows, block_rows)
    slot_ids = family_slots(own_fam.reshape(1, block_rows))[0]
    dest_cols = own_fam * CAP + slot_ids
    select = (dest_cols[:, None] == jnp.arange(FAM * CAP, dtype=jnp.int32)[None, :]).astype(
        jnp.bfloat16
    )
    packed = jnp.dot(select.T, own_rows, preferred_element_type=jnp.float32).astype(jnp.bfloat16)
    packed = packed.reshape(FAM, CAP, feat_width)
    by_family = lax.all_to_all(packed, "ty", split_axis=0, concat_axis=0, tiled=True)
    received = lax.all_gather(by_family, "tz")
    x_full = x_in.astype(jnp.float32)
    b_full = b_in.astype(jnp.float32)
    c_full = c_in.astype(jnp.float32)
    log_sums = jnp.cumsum(-step_size * a_rate[None, None, :], axis=0)
    counts = jnp.cumsum(doc_start, axis=0)
    same_end = (counts == counts[-1][None, :]).astype(jnp.float32)
    to_end = jnp.exp(log_sums[-1][None] - log_sums) * same_end[:, :, None]
    from_start = jnp.exp(log_sums) * (counts == 0).astype(jnp.float32)[:, :, None]
    through = jnp.exp(log_sums[-1]) * (counts[-1] == 0).astype(jnp.float32)[:, None]
    inputs = step_size[..., None] * x_full
    local_state = jnp.einsum("jbh,jbhp,jbhn->bhpn", to_end, inputs, b_full, precision=HIGH)
    place = lax.axis_index("seq")
    through_hi = through.astype(jnp.bfloat16)
    through_lo = (through - through_hi.astype(jnp.float32)).astype(jnp.bfloat16)
    edge = local_state.shape[-1]
    packed_state = jnp.concatenate(
        [
            local_state.astype(jnp.bfloat16),
            jnp.broadcast_to(through_hi[:, :, None, None], through.shape + (1, edge)),
            jnp.broadcast_to(through_lo[:, :, None, None], through.shape + (1, edge)),
        ],
        axis=2,
    )
    gathered = lax.all_gather(packed_state, "seq")
    rows = local_state.shape[2]
    through_all = gathered[:, :, :, rows, 0].astype(jnp.float32) + gathered[
        :, :, :, rows + 1, 0
    ].astype(jnp.float32)
    slots_all = n_z * n_y * CAP
    received, gathered = lax.optimization_barrier((received, gathered))
    received = received.reshape(slots_all, feat_width)
    weights = teacher_proj[0]
    partial_value = jnp.dot(received, weights, preferred_element_type=jnp.float32)
    sq_sums = jnp.sum(jnp.square(received.astype(jnp.float32)), axis=1)
    width = partial_value.shape[-1]
    group = n_y * CAP
    partial_value = partial_value.reshape(n_z, group, width)
    sq_all = sq_sums.reshape(n_z, group)
    sq_hi = sq_all.astype(jnp.bfloat16)
    sq_lo = (sq_all - sq_hi.astype(jnp.float32)).astype(jnp.bfloat16)
    sq_row = jnp.concatenate([sq_hi, sq_lo], axis=1)[:, None, :]
    outbound = jnp.concatenate([partial_value.astype(jnp.bfloat16), sq_row], axis=1)
    inbound = lax.all_to_all(outbound, "seq", split_axis=0, concat_axis=0, tiled=True)
    summed = jnp.sum(inbound.astype(jnp.float32), axis=0)
    sq_total = summed[group, :group] + summed[group, group : 2 * group]
    row_scale = lax.rsqrt(sq_total / TD + EPS)
    scaled = (summed[:group] * row_scale[:, None]).astype(jnp.bfloat16)
    scaled = scaled.reshape(group, heads_all, -1)
    cols = scaled.shape[-1]
    outgoing = scaled.transpose(1, 0, 2)
    arrived = lax.all_to_all(outgoing, TEACH, split_axis=0, concat_axis=0, tiled=True)
    arrived = arrived.reshape(n_z, n_y, n_y * CAP, cols)
    table = arrived.transpose(1, 2, 0, 3).reshape(n_y * n_y * CAP, n_z * cols)

    shard_rows = n_y * block_rows
    shard_fam = lax.dynamic_slice_in_dim(
        fam_all, lax.axis_index("seq") * shard_rows, shard_rows
    ).reshape(n_y, block_rows)
    shard_slots = family_slots(shard_fam)
    sources = jnp.arange(n_y, dtype=jnp.int32)[:, None]
    row_index = ((shard_fam * n_y + sources) * CAP + shard_slots).reshape(shard_rows)
    picked = jnp.take(table, row_index, axis=0)
    target = picked.reshape(n_y * block_pos, batch_n, 1, P_SIZE)

    state_in = combine(chain_weights(through_all, place, False), gathered[:, :, :, :rows])
    decay_mat = decay_matrix(log_sums, counts)
    scores = jnp.einsum("ibhn,jbhn->bhij", c_in, b_in, preferred_element_type=jnp.float32)
    mixing = decay_mat * scores
    output = jnp.einsum("bhij,jbhp->ibhp", mixing, inputs, precision=QUADRATIC)
    output = output + from_start[..., None] * jnp.einsum(
        "ibhn,bhpn->ibhp", c_full, state_in, precision=HIGH
    )
    output = output + skip_gain[None, None, :, None] * x_full
    residual = output - target.astype(jnp.float32)
    local_adjoint = jnp.einsum("ibh,ibhn,ibhp->bhnp", from_start, c_full, residual, precision=HIGH)
    adjoint_all = lax.all_to_all(
        jnp.broadcast_to(local_adjoint.astype(jnp.bfloat16)[None], (seq_n,) + local_adjoint.shape),
        "seq",
        split_axis=0,
        concat_axis=0,
        tiled=True,
    )
    adjoint_in = combine(chain_weights(through_all, place, True), adjoint_all)
    grad_u = jnp.einsum("bhij,ibhp->jbhp", mixing, residual, precision=QUADRATIC)
    grad_u = grad_u + to_end[..., None] * jnp.einsum(
        "jbhn,bhnp->jbhp", b_full, adjoint_in, precision=HIGH
    )
    grad_x = step_size[..., None] * grad_u + skip_gain[None, None, :, None] * residual
    pair = decay_mat * jnp.einsum("ibhp,jbhp->bhij", residual, inputs, precision=QUADRATIC)
    grad_b = jnp.einsum("bhij,ibhn->jbhn", pair, c_full, precision=QUADRATIC)
    grad_b = grad_b + to_end[..., None] * jnp.einsum(
        "jbhp,bhnp->jbhn", inputs, adjoint_in, precision=HIGH
    )
    grad_c = jnp.einsum("bhij,jbhn->ibhn", pair, b_full, precision=QUADRATIC)
    grad_c = grad_c + from_start[..., None] * jnp.einsum(
        "ibhp,bhpn->ibhn", residual, state_in, precision=HIGH
    )
    return (grad_x.astype(jnp.bfloat16), grad_b.astype(jnp.bfloat16), grad_c.astype(jnp.bfloat16))


def solution(mesh):
    teach_n, seq_n = mesh.devices.shape
    n_y = FAM
    n_z = teach_n // n_y
    assert n_z == seq_n
    split = Mesh(mesh.devices.reshape(n_z, n_y, seq_n), ("tz", "ty", "seq"))
    placed = (
        P(TEACH, None, "seq"),
        P(TEACH, "seq", None),
        P(),
        P("seq", None, TEACH, None),
        P("seq", None, TEACH, None),
        P("seq", None, TEACH, None),
        P("seq", None, TEACH),
        P("seq", None),
        P(TEACH),
        P(TEACH),
    )
    return jax.shard_map(
        per_device,
        mesh=split,
        in_specs=placed,
        out_specs=(
            P("seq", None, TEACH, None),
            P("seq", None, TEACH, None),
            P("seq", None, TEACH, None),
        ),
        check_vma=False,
    )
```

```python
import jax
import jax.numpy as jnp
from jax import lax
from jax.sharding import Mesh
from jax.sharding import PartitionSpec as P

TD = 5120
P_SIZE = 64
FAM = 8
CAP = 32


EPS = 1e-06
HIGH = lax.Precision.HIGHEST
QUADRATIC = lax.Precision.HIGH
TEACH = ("tz", "ty")


def family_slots(fam_block):
    onehot = (fam_block[..., None] == jnp.arange(FAM, dtype=jnp.int32)[None, None, :]).astype(
        jnp.int32
    )
    before = jnp.cumsum(onehot, axis=1) - onehot
    return jnp.sum(before * onehot, axis=2)


def decay_matrix(log_sums, counts):
    places = jnp.arange(log_sums.shape[0])
    lower = places[:, None] >= places[None, :]
    same_doc = counts.T[:, :, None] == counts.T[:, None, :]
    keep_mask = (lower[None] & same_doc)[:, None]
    sums = log_sums.transpose(1, 2, 0)
    gaps = sums[:, :, :, None] - sums[:, :, None, :]
    return jnp.where(keep_mask, jnp.exp(jnp.where(keep_mask, gaps, 0.0)), 0.0)


def chain_weights(through_all, place, backward):
    count = through_all.shape[0]
    blocks = jnp.arange(count)
    s2 = blocks[:, None]
    s3 = blocks[None, :]
    if backward:
        used = (s3 > place) & (s3 < s2)
        live = blocks > place
    else:
        used = (s3 > s2) & (s3 < place)
        live = blocks < place
    factors = jnp.where(used[:, :, None, None], through_all[None], 1.0)
    weights = jnp.prod(factors, axis=1)
    return jnp.where(live[:, None, None], weights, 0.0)


def combine(weights, local_all):
    return jnp.sum(weights[:, :, :, None, None] * local_all.astype(jnp.float32), axis=0)


def ring_gather(x, axis):
    count = lax.axis_size(axis)
    ahead = [(i, (i + 1) % count) for i in range(count)]
    behind = [(i, (i - 1) % count) for i in range(count)]
    later = [None] * count
    later[0] = x
    cw = x
    ccw = x
    for hop in range(1, count // 2 + 1):
        cw = lax.ppermute(cw, axis, ahead)
        later[count - hop] = cw
        if hop < count - hop:
            ccw = lax.ppermute(ccw, axis, behind)
            later[hop] = ccw
    rel = jnp.stack(later)
    place = lax.axis_index(axis)
    doubled = jnp.concatenate([rel, rel])
    return lax.dynamic_slice_in_dim(doubled, (count - place) % count, count)


def per_device(
    teacher_in, teacher_proj, family, x_in, b_in, c_in, step_size, doc_start, a_rate, skip_gain
):
    n_z = lax.axis_size("tz")
    n_y = lax.axis_size("ty")
    seq_n = lax.axis_size("seq")
    teach_n = n_z * n_y
    heads_all = teach_n * x_in.shape[2]
    block_pos = teacher_in.shape[0]
    batch_n = teacher_in.shape[1]
    feat_width = teacher_in.shape[2]
    block_rows = block_pos * batch_n
    source = lax.axis_index("tz") * n_y + lax.axis_index("ty")
    fam_all = family.reshape(family.shape[0] * family.shape[1])

    own_rows = teacher_in.reshape(block_rows, feat_width)
    own_fam = lax.dynamic_slice_in_dim(fam_all, source * block_rows, block_rows)
    slot_ids = family_slots(own_fam.reshape(1, block_rows))[0]
    dest_cols = own_fam * CAP + slot_ids
    select = (dest_cols[:, None] == jnp.arange(FAM * CAP, dtype=jnp.int32)[None, :]).astype(
        jnp.bfloat16
    )
    packed = jnp.dot(select.T, own_rows, preferred_element_type=jnp.float32).astype(jnp.bfloat16)
    packed = packed.reshape(FAM, CAP, feat_width)
    by_family = lax.all_to_all(packed, "ty", split_axis=0, concat_axis=0, tiled=True)
    received = ring_gather(by_family, "tz")
    x_full = x_in.astype(jnp.float32)
    b_full = b_in.astype(jnp.float32)
    c_full = c_in.astype(jnp.float32)
    log_sums = jnp.cumsum(-step_size * a_rate[None, None, :], axis=0)
    counts = jnp.cumsum(doc_start, axis=0)
    same_end = (counts == counts[-1][None, :]).astype(jnp.float32)
    to_end = jnp.exp(log_sums[-1][None] - log_sums) * same_end[:, :, None]
    from_start = jnp.exp(log_sums) * (counts == 0).astype(jnp.float32)[:, :, None]
    through = jnp.exp(log_sums[-1]) * (counts[-1] == 0).astype(jnp.float32)[:, None]
    inputs = step_size[..., None] * x_full
    local_state = jnp.einsum("jbh,jbhp,jbhn->bhpn", to_end, inputs, b_full, precision=HIGH)
    place = lax.axis_index("seq")
    through_hi = through.astype(jnp.bfloat16)
    through_lo = (through - through_hi.astype(jnp.float32)).astype(jnp.bfloat16)
    edge = local_state.shape[-1]
    packed_state = jnp.concatenate(
        [
            local_state.astype(jnp.bfloat16),
            jnp.broadcast_to(through_hi[:, :, None, None], through.shape + (1, edge)),
            jnp.broadcast_to(through_lo[:, :, None, None], through.shape + (1, edge)),
        ],
        axis=2,
    )
    gathered = lax.all_gather(packed_state, "seq")
    rows = local_state.shape[2]
    through_all = gathered[:, :, :, rows, 0].astype(jnp.float32) + gathered[
        :, :, :, rows + 1, 0
    ].astype(jnp.float32)
    slots_all = n_z * n_y * CAP
    received, gathered = lax.optimization_barrier((received, gathered))
    received = received.reshape(slots_all, feat_width)
    weights = teacher_proj[0]
    partial_value = jnp.dot(received, weights, preferred_element_type=jnp.float32)
    sq_sums = jnp.sum(jnp.square(received.astype(jnp.float32)), axis=1)
    width = partial_value.shape[-1]
    group = n_y * CAP
    partial_value = partial_value.reshape(n_z, group, width)
    sq_all = sq_sums.reshape(n_z, group)
    sq_hi = sq_all.astype(jnp.bfloat16)
    sq_lo = (sq_all - sq_hi.astype(jnp.float32)).astype(jnp.bfloat16)
    sq_row = jnp.concatenate([sq_hi, sq_lo], axis=1)[:, None, :]
    outbound = jnp.concatenate([partial_value.astype(jnp.bfloat16), sq_row], axis=1)
    inbound = lax.all_to_all(outbound, "seq", split_axis=0, concat_axis=0, tiled=True)
    summed = jnp.sum(inbound.astype(jnp.float32), axis=0)
    sq_total = summed[group, :group] + summed[group, group : 2 * group]
    row_scale = lax.rsqrt(sq_total / TD + EPS)
    scaled = (summed[:group] * row_scale[:, None]).astype(jnp.bfloat16)
    scaled = scaled.reshape(group, heads_all, -1)
    cols = scaled.shape[-1]
    outgoing = scaled.transpose(1, 0, 2)
    arrived = lax.all_to_all(outgoing, TEACH, split_axis=0, concat_axis=0, tiled=True)
    arrived = arrived.reshape(n_z, n_y, n_y * CAP, cols)
    table = arrived.transpose(1, 2, 0, 3).reshape(n_y * n_y * CAP, n_z * cols)

    shard_rows = n_y * block_rows
    shard_fam = lax.dynamic_slice_in_dim(
        fam_all, lax.axis_index("seq") * shard_rows, shard_rows
    ).reshape(n_y, block_rows)
    shard_slots = family_slots(shard_fam)
    sources = jnp.arange(n_y, dtype=jnp.int32)[:, None]
    row_index = ((shard_fam * n_y + sources) * CAP + shard_slots).reshape(shard_rows)
    picked = jnp.take(table, row_index, axis=0)
    target = picked.reshape(n_y * block_pos, batch_n, 1, P_SIZE)

    state_in = combine(chain_weights(through_all, place, False), gathered[:, :, :, :rows])
    decay_mat = decay_matrix(log_sums, counts)
    scores = jnp.einsum("ibhn,jbhn->bhij", c_in, b_in, preferred_element_type=jnp.float32)
    mixing = decay_mat * scores
    output = jnp.einsum("bhij,jbhp->ibhp", mixing, inputs, precision=QUADRATIC)
    output = output + from_start[..., None] * jnp.einsum(
        "ibhn,bhpn->ibhp", c_full, state_in, precision=HIGH
    )
    output = output + skip_gain[None, None, :, None] * x_full
    residual = output - target.astype(jnp.float32)
    local_adjoint = jnp.einsum("ibh,ibhn,ibhp->bhnp", from_start, c_full, residual, precision=HIGH)
    adjoint_all = lax.all_to_all(
        jnp.broadcast_to(local_adjoint.astype(jnp.bfloat16)[None], (seq_n,) + local_adjoint.shape),
        "seq",
        split_axis=0,
        concat_axis=0,
        tiled=True,
    )
    adjoint_in = combine(chain_weights(through_all, place, True), adjoint_all)
    grad_u = jnp.einsum("bhij,ibhp->jbhp", mixing, residual, precision=QUADRATIC)
    grad_u = grad_u + to_end[..., None] * jnp.einsum(
        "jbhn,bhnp->jbhp", b_full, adjoint_in, precision=HIGH
    )
    grad_x = step_size[..., None] * grad_u + skip_gain[None, None, :, None] * residual
    pair = decay_mat * jnp.einsum("ibhp,jbhp->bhij", residual, inputs, precision=QUADRATIC)
    grad_b = jnp.einsum("bhij,ibhn->jbhn", pair, c_full, precision=QUADRATIC)
    grad_b = grad_b + to_end[..., None] * jnp.einsum(
        "jbhp,bhnp->jbhn", inputs, adjoint_in, precision=HIGH
    )
    grad_c = jnp.einsum("bhij,jbhn->ibhn", pair, b_full, precision=QUADRATIC)
    grad_c = grad_c + from_start[..., None] * jnp.einsum(
        "ibhp,bhpn->ibhn", residual, state_in, precision=HIGH
    )
    return (grad_x.astype(jnp.bfloat16), grad_b.astype(jnp.bfloat16), grad_c.astype(jnp.bfloat16))


def solution(mesh):
    teach_n, seq_n = mesh.devices.shape
    n_y = FAM
    n_z = teach_n // n_y
    assert n_z == seq_n
    split = Mesh(mesh.devices.reshape(n_z, n_y, seq_n), ("tz", "ty", "seq"))
    placed = (
        P(TEACH, None, "seq"),
        P(TEACH, "seq", None),
        P(),
        P("seq", None, TEACH, None),
        P("seq", None, TEACH, None),
        P("seq", None, TEACH, None),
        P("seq", None, TEACH),
        P("seq", None),
        P(TEACH),
        P(TEACH),
    )
    return jax.shard_map(
        per_device,
        mesh=split,
        in_specs=placed,
        out_specs=(
            P("seq", None, TEACH, None),
            P("seq", None, TEACH, None),
            P("seq", None, TEACH, None),
        ),
        check_vma=False,
    )
```

```python
import jax
import jax.numpy as jnp
from jax import lax
from jax.sharding import Mesh
from jax.sharding import PartitionSpec as P

TD = 5120
P_SIZE = 64
FAM = 8
CAP = 32


EPS = 1e-06
HIGH = lax.Precision.HIGHEST
QUADRATIC = lax.Precision.HIGH
TEACH = ("tz", "ty")


def family_slots(fam_block):
    onehot = (fam_block[..., None] == jnp.arange(FAM, dtype=jnp.int32)[None, None, :]).astype(
        jnp.int32
    )
    before = jnp.cumsum(onehot, axis=1) - onehot
    return jnp.sum(before * onehot, axis=2)


def decay_matrix(log_sums, counts):
    places = jnp.arange(log_sums.shape[0])
    lower = places[:, None] >= places[None, :]
    same_doc = counts.T[:, :, None] == counts.T[:, None, :]
    keep_mask = (lower[None] & same_doc)[:, None]
    sums = log_sums.transpose(1, 2, 0)
    gaps = sums[:, :, :, None] - sums[:, :, None, :]
    return jnp.where(keep_mask, jnp.exp(jnp.where(keep_mask, gaps, 0.0)), 0.0)


def chain_weights(through_all, place, backward):
    count = through_all.shape[0]
    blocks = jnp.arange(count)
    s2 = blocks[:, None]
    s3 = blocks[None, :]
    if backward:
        used = (s3 > place) & (s3 < s2)
        live = blocks > place
    else:
        used = (s3 > s2) & (s3 < place)
        live = blocks < place
    factors = jnp.where(used[:, :, None, None], through_all[None], 1.0)
    weights = jnp.prod(factors, axis=1)
    return jnp.where(live[:, None, None], weights, 0.0)


def combine(weights, local_all):
    return jnp.sum(weights[:, :, :, None, None] * local_all.astype(jnp.float32), axis=0)


def ring_gather(x, axis):
    count = lax.axis_size(axis)
    ahead = [(i, (i + 1) % count) for i in range(count)]
    behind = [(i, (i - 1) % count) for i in range(count)]
    later = [None] * count
    later[0] = x
    cw = x
    ccw = x
    for hop in range(1, count // 2 + 1):
        cw = lax.ppermute(cw, axis, ahead)
        later[count - hop] = cw
        if hop < count - hop:
            ccw = lax.ppermute(ccw, axis, behind)
            later[hop] = ccw
    rel = jnp.stack(later)
    place = lax.axis_index(axis)
    doubled = jnp.concatenate([rel, rel])
    return lax.dynamic_slice_in_dim(doubled, (count - place) % count, count)


def per_device(
    teacher_in, teacher_proj, family, x_in, b_in, c_in, step_size, doc_start, a_rate, skip_gain
):
    n_z = lax.axis_size("tz")
    n_y = lax.axis_size("ty")
    seq_n = lax.axis_size("seq")
    teach_n = n_z * n_y
    heads_all = teach_n * x_in.shape[2]
    block_pos = teacher_in.shape[0]
    batch_n = teacher_in.shape[1]
    feat_width = teacher_in.shape[2]
    block_rows = block_pos * batch_n
    source = lax.axis_index("tz") * n_y + lax.axis_index("ty")
    fam_all = family.reshape(family.shape[0] * family.shape[1])

    own_rows = teacher_in.reshape(block_rows, feat_width)
    own_fam = lax.dynamic_slice_in_dim(fam_all, source * block_rows, block_rows)
    slot_ids = family_slots(own_fam.reshape(1, block_rows))[0]
    dest_cols = own_fam * CAP + slot_ids
    select = (dest_cols[:, None] == jnp.arange(FAM * CAP, dtype=jnp.int32)[None, :]).astype(
        jnp.bfloat16
    )
    packed = jnp.dot(select.T, own_rows, preferred_element_type=jnp.float32).astype(jnp.bfloat16)
    packed = packed.reshape(FAM, CAP, feat_width)
    by_family = lax.all_to_all(packed, "ty", split_axis=0, concat_axis=0, tiled=True)
    received = ring_gather(by_family, "tz")
    x_full = x_in.astype(jnp.float32)
    b_full = b_in.astype(jnp.float32)
    c_full = c_in.astype(jnp.float32)
    log_sums = jnp.cumsum(-step_size * a_rate[None, None, :], axis=0)
    counts = jnp.cumsum(doc_start, axis=0)
    same_end = (counts == counts[-1][None, :]).astype(jnp.float32)
    to_end = jnp.exp(log_sums[-1][None] - log_sums) * same_end[:, :, None]
    from_start = jnp.exp(log_sums) * (counts == 0).astype(jnp.float32)[:, :, None]
    through = jnp.exp(log_sums[-1]) * (counts[-1] == 0).astype(jnp.float32)[:, None]
    inputs = step_size[..., None] * x_full
    local_state = jnp.einsum("jbh,jbhp,jbhn->bhpn", to_end, inputs, b_full, precision=HIGH)
    place = lax.axis_index("seq")
    through_hi = through.astype(jnp.bfloat16)
    through_lo = (through - through_hi.astype(jnp.float32)).astype(jnp.bfloat16)
    edge = local_state.shape[-1]
    packed_state = jnp.concatenate(
        [
            local_state.astype(jnp.bfloat16),
            jnp.broadcast_to(through_hi[:, :, None, None], through.shape + (1, edge)),
            jnp.broadcast_to(through_lo[:, :, None, None], through.shape + (1, edge)),
        ],
        axis=2,
    )
    packed_state = lax.optimization_barrier((packed_state, received))[0]
    gathered = lax.all_gather(packed_state, "seq")
    rows = local_state.shape[2]
    through_all = gathered[:, :, :, rows, 0].astype(jnp.float32) + gathered[
        :, :, :, rows + 1, 0
    ].astype(jnp.float32)
    slots_all = n_z * n_y * CAP
    received = received.reshape(slots_all, feat_width)
    weights = teacher_proj[0]
    partial_value = jnp.dot(received, weights, preferred_element_type=jnp.float32)
    sq_sums = jnp.sum(jnp.square(received.astype(jnp.float32)), axis=1)
    width = partial_value.shape[-1]
    group = n_y * CAP
    partial_value = partial_value.reshape(n_z, group, width)
    sq_all = sq_sums.reshape(n_z, group)
    sq_hi = sq_all.astype(jnp.bfloat16)
    sq_lo = (sq_all - sq_hi.astype(jnp.float32)).astype(jnp.bfloat16)
    sq_row = jnp.concatenate([sq_hi, sq_lo], axis=1)[:, None, :]
    outbound = jnp.concatenate([partial_value.astype(jnp.bfloat16), sq_row], axis=1)
    inbound = lax.all_to_all(outbound, "seq", split_axis=0, concat_axis=0, tiled=True)
    summed = jnp.sum(inbound.astype(jnp.float32), axis=0)
    sq_total = summed[group, :group] + summed[group, group : 2 * group]
    row_scale = lax.rsqrt(sq_total / TD + EPS)
    scaled = (summed[:group] * row_scale[:, None]).astype(jnp.bfloat16)
    scaled = scaled.reshape(group, heads_all, -1)
    cols = scaled.shape[-1]
    outgoing = scaled.transpose(1, 0, 2)
    arrived = lax.all_to_all(outgoing, TEACH, split_axis=0, concat_axis=0, tiled=True)
    arrived = arrived.reshape(n_z, n_y, n_y * CAP, cols)
    table = arrived.transpose(1, 2, 0, 3).reshape(n_y * n_y * CAP, n_z * cols)

    shard_rows = n_y * block_rows
    shard_fam = lax.dynamic_slice_in_dim(
        fam_all, lax.axis_index("seq") * shard_rows, shard_rows
    ).reshape(n_y, block_rows)
    shard_slots = family_slots(shard_fam)
    sources = jnp.arange(n_y, dtype=jnp.int32)[:, None]
    row_index = ((shard_fam * n_y + sources) * CAP + shard_slots).reshape(shard_rows)
    picked = jnp.take(table, row_index, axis=0)
    target = picked.reshape(n_y * block_pos, batch_n, 1, P_SIZE)

    state_in = combine(chain_weights(through_all, place, False), gathered[:, :, :, :rows])
    decay_mat = decay_matrix(log_sums, counts)
    scores = jnp.einsum("ibhn,jbhn->bhij", c_in, b_in, preferred_element_type=jnp.float32)
    mixing = decay_mat * scores
    output = jnp.einsum("bhij,jbhp->ibhp", mixing, inputs, precision=QUADRATIC)
    output = output + from_start[..., None] * jnp.einsum(
        "ibhn,bhpn->ibhp", c_full, state_in, precision=HIGH
    )
    output = output + skip_gain[None, None, :, None] * x_full
    residual = output - target.astype(jnp.float32)
    local_adjoint = jnp.einsum("ibh,ibhn,ibhp->bhnp", from_start, c_full, residual, precision=HIGH)
    adjoint_all = lax.all_to_all(
        jnp.broadcast_to(local_adjoint.astype(jnp.bfloat16)[None], (seq_n,) + local_adjoint.shape),
        "seq",
        split_axis=0,
        concat_axis=0,
        tiled=True,
    )
    adjoint_in = combine(chain_weights(through_all, place, True), adjoint_all)
    grad_u = jnp.einsum("bhij,ibhp->jbhp", mixing, residual, precision=QUADRATIC)
    grad_u = grad_u + to_end[..., None] * jnp.einsum(
        "jbhn,bhnp->jbhp", b_full, adjoint_in, precision=HIGH
    )
    grad_x = step_size[..., None] * grad_u + skip_gain[None, None, :, None] * residual
    pair = decay_mat * jnp.einsum("ibhp,jbhp->bhij", residual, inputs, precision=QUADRATIC)
    grad_b = jnp.einsum("bhij,ibhn->jbhn", pair, c_full, precision=QUADRATIC)
    grad_b = grad_b + to_end[..., None] * jnp.einsum(
        "jbhp,bhnp->jbhn", inputs, adjoint_in, precision=HIGH
    )
    grad_c = jnp.einsum("bhij,jbhn->ibhn", pair, b_full, precision=QUADRATIC)
    grad_c = grad_c + from_start[..., None] * jnp.einsum(
        "ibhp,bhpn->ibhn", residual, state_in, precision=HIGH
    )
    return (grad_x.astype(jnp.bfloat16), grad_b.astype(jnp.bfloat16), grad_c.astype(jnp.bfloat16))


def solution(mesh):
    teach_n, seq_n = mesh.devices.shape
    n_y = FAM
    n_z = teach_n // n_y
    assert n_z == seq_n
    split = Mesh(mesh.devices.reshape(n_z, n_y, seq_n), ("tz", "ty", "seq"))
    placed = (
        P(TEACH, None, "seq"),
        P(TEACH, "seq", None),
        P(),
        P("seq", None, TEACH, None),
        P("seq", None, TEACH, None),
        P("seq", None, TEACH, None),
        P("seq", None, TEACH),
        P("seq", None),
        P(TEACH),
        P(TEACH),
    )
    return jax.shard_map(
        per_device,
        mesh=split,
        in_specs=placed,
        out_specs=(
            P("seq", None, TEACH, None),
            P("seq", None, TEACH, None),
            P("seq", None, TEACH, None),
        ),
        check_vma=False,
    )
```

```python
import jax
import jax.numpy as jnp
from jax import lax
from jax.sharding import Mesh
from jax.sharding import PartitionSpec as P

TD = 5120
P_SIZE = 64
FAM = 8
CAP = 32


EPS = 1e-06
HIGH = lax.Precision.HIGHEST
QUADRATIC = lax.Precision.HIGH
TEACH = ("tz", "ty")


def family_slots(fam_block):
    onehot = (fam_block[..., None] == jnp.arange(FAM, dtype=jnp.int32)[None, None, :]).astype(
        jnp.int32
    )
    before = jnp.cumsum(onehot, axis=1) - onehot
    return jnp.sum(before * onehot, axis=2)


def decay_matrix(log_sums, counts):
    places = jnp.arange(log_sums.shape[0])
    lower = places[:, None] >= places[None, :]
    same_doc = counts.T[:, :, None] == counts.T[:, None, :]
    keep_mask = (lower[None] & same_doc)[:, None]
    sums = log_sums.transpose(1, 2, 0)
    gaps = sums[:, :, :, None] - sums[:, :, None, :]
    return jnp.where(keep_mask, jnp.exp(jnp.where(keep_mask, gaps, 0.0)), 0.0)


def chain_weights(through_all, place, backward):
    count = through_all.shape[0]
    blocks = jnp.arange(count)
    s2 = blocks[:, None]
    s3 = blocks[None, :]
    if backward:
        used = (s3 > place) & (s3 < s2)
        live = blocks > place
    else:
        used = (s3 > s2) & (s3 < place)
        live = blocks < place
    factors = jnp.where(used[:, :, None, None], through_all[None], 1.0)
    weights = jnp.prod(factors, axis=1)
    return jnp.where(live[:, None, None], weights, 0.0)


def combine(weights, local_all):
    return jnp.sum(weights[:, :, :, None, None] * local_all.astype(jnp.float32), axis=0)


def ring_gather(x, axis):
    count = lax.axis_size(axis)
    ahead = [(i, (i + 1) % count) for i in range(count)]
    behind = [(i, (i - 1) % count) for i in range(count)]
    later = [None] * count
    later[0] = x
    cw = x
    ccw = x
    for hop in range(1, count // 2 + 1):
        cw = lax.ppermute(cw, axis, ahead)
        later[count - hop] = cw
        if hop < count - hop:
            ccw = lax.ppermute(ccw, axis, behind)
            later[hop] = ccw
    rel = jnp.stack(later)
    place = lax.axis_index(axis)
    doubled = jnp.concatenate([rel, rel])
    return lax.dynamic_slice_in_dim(doubled, (count - place) % count, count)


def per_device(
    teacher_in, teacher_proj, family, x_in, b_in, c_in, step_size, doc_start, a_rate, skip_gain
):
    n_z = lax.axis_size("tz")
    n_y = lax.axis_size("ty")
    seq_n = lax.axis_size("seq")
    teach_n = n_z * n_y
    heads_all = teach_n * x_in.shape[2]
    block_pos = teacher_in.shape[0]
    batch_n = teacher_in.shape[1]
    feat_width = teacher_in.shape[2]
    block_rows = block_pos * batch_n
    source = lax.axis_index("tz") * n_y + lax.axis_index("ty")
    fam_all = family.reshape(family.shape[0] * family.shape[1])

    own_rows = teacher_in.reshape(block_rows, feat_width)
    own_fam = lax.dynamic_slice_in_dim(fam_all, source * block_rows, block_rows)
    slot_ids = family_slots(own_fam.reshape(1, block_rows))[0]
    dest_cols = own_fam * CAP + slot_ids
    select = (dest_cols[:, None] == jnp.arange(FAM * CAP, dtype=jnp.int32)[None, :]).astype(
        jnp.bfloat16
    )
    packed = jnp.dot(select.T, own_rows, preferred_element_type=jnp.float32).astype(jnp.bfloat16)
    packed = packed.reshape(FAM, CAP, feat_width)
    by_family = lax.all_to_all(packed, "ty", split_axis=0, concat_axis=0, tiled=True)
    received = ring_gather(by_family, "tz")
    x_full = x_in.astype(jnp.float32)
    b_full = b_in.astype(jnp.float32)
    c_full = c_in.astype(jnp.float32)
    log_sums = jnp.cumsum(-step_size * a_rate[None, None, :], axis=0)
    counts = jnp.cumsum(doc_start, axis=0)
    same_end = (counts == counts[-1][None, :]).astype(jnp.float32)
    to_end = jnp.exp(log_sums[-1][None] - log_sums) * same_end[:, :, None]
    from_start = jnp.exp(log_sums) * (counts == 0).astype(jnp.float32)[:, :, None]
    through = jnp.exp(log_sums[-1]) * (counts[-1] == 0).astype(jnp.float32)[:, None]
    inputs = step_size[..., None] * x_full
    local_state = jnp.einsum("jbh,jbhp,jbhn->bhpn", to_end, inputs, b_full, precision=HIGH)
    place = lax.axis_index("seq")
    through_hi = through.astype(jnp.bfloat16)
    through_lo = (through - through_hi.astype(jnp.float32)).astype(jnp.bfloat16)
    edge = local_state.shape[-1]
    packed_state = jnp.concatenate(
        [
            local_state.astype(jnp.bfloat16),
            jnp.broadcast_to(through_hi[:, :, None, None], through.shape + (1, edge)),
            jnp.broadcast_to(through_lo[:, :, None, None], through.shape + (1, edge)),
        ],
        axis=2,
    )
    gathered = lax.all_to_all(
        jnp.broadcast_to(packed_state[None], (seq_n,) + packed_state.shape),
        "seq",
        split_axis=0,
        concat_axis=0,
        tiled=True,
    )
    rows = local_state.shape[2]
    through_all = gathered[:, :, :, rows, 0].astype(jnp.float32) + gathered[
        :, :, :, rows + 1, 0
    ].astype(jnp.float32)
    slots_all = n_z * n_y * CAP
    received = received.reshape(slots_all, feat_width)
    weights = teacher_proj[0]
    partial_value = jnp.dot(received, weights, preferred_element_type=jnp.float32)
    sq_sums = jnp.sum(jnp.square(received.astype(jnp.float32)), axis=1)
    width = partial_value.shape[-1]
    group = n_y * CAP
    partial_value = partial_value.reshape(n_z, group, width)
    sq_all = sq_sums.reshape(n_z, group)
    sq_hi = sq_all.astype(jnp.bfloat16)
    sq_lo = (sq_all - sq_hi.astype(jnp.float32)).astype(jnp.bfloat16)
    sq_row = jnp.concatenate([sq_hi, sq_lo], axis=1)[:, None, :]
    outbound = jnp.concatenate([partial_value.astype(jnp.bfloat16), sq_row], axis=1)
    inbound = lax.all_to_all(outbound, "seq", split_axis=0, concat_axis=0, tiled=True)
    summed = jnp.sum(inbound.astype(jnp.float32), axis=0)
    sq_total = summed[group, :group] + summed[group, group : 2 * group]
    row_scale = lax.rsqrt(sq_total / TD + EPS)
    scaled = (summed[:group] * row_scale[:, None]).astype(jnp.bfloat16)
    scaled = scaled.reshape(group, heads_all, -1)
    cols = scaled.shape[-1]
    outgoing = scaled.transpose(1, 0, 2)
    arrived = lax.all_to_all(outgoing, TEACH, split_axis=0, concat_axis=0, tiled=True)
    arrived = arrived.reshape(n_z, n_y, n_y * CAP, cols)
    table = arrived.transpose(1, 2, 0, 3).reshape(n_y * n_y * CAP, n_z * cols)

    shard_rows = n_y * block_rows
    shard_fam = lax.dynamic_slice_in_dim(
        fam_all, lax.axis_index("seq") * shard_rows, shard_rows
    ).reshape(n_y, block_rows)
    shard_slots = family_slots(shard_fam)
    sources = jnp.arange(n_y, dtype=jnp.int32)[:, None]
    row_index = ((shard_fam * n_y + sources) * CAP + shard_slots).reshape(shard_rows)
    picked = jnp.take(table, row_index, axis=0)
    target = picked.reshape(n_y * block_pos, batch_n, 1, P_SIZE)

    state_in = combine(chain_weights(through_all, place, False), gathered[:, :, :, :rows])
    decay_mat = decay_matrix(log_sums, counts)
    scores = jnp.einsum("ibhn,jbhn->bhij", c_in, b_in, preferred_element_type=jnp.float32)
    mixing = decay_mat * scores
    output = jnp.einsum("bhij,jbhp->ibhp", mixing, inputs, precision=QUADRATIC)
    output = output + from_start[..., None] * jnp.einsum(
        "ibhn,bhpn->ibhp", c_full, state_in, precision=HIGH
    )
    output = output + skip_gain[None, None, :, None] * x_full
    residual = output - target.astype(jnp.float32)
    local_adjoint = jnp.einsum("ibh,ibhn,ibhp->bhnp", from_start, c_full, residual, precision=HIGH)
    adjoint_all = lax.all_to_all(
        jnp.broadcast_to(local_adjoint.astype(jnp.bfloat16)[None], (seq_n,) + local_adjoint.shape),
        "seq",
        split_axis=0,
        concat_axis=0,
        tiled=True,
    )
    adjoint_in = combine(chain_weights(through_all, place, True), adjoint_all)
    grad_u = jnp.einsum("bhij,ibhp->jbhp", mixing, residual, precision=QUADRATIC)
    grad_u = grad_u + to_end[..., None] * jnp.einsum(
        "jbhn,bhnp->jbhp", b_full, adjoint_in, precision=HIGH
    )
    grad_x = step_size[..., None] * grad_u + skip_gain[None, None, :, None] * residual
    pair = decay_mat * jnp.einsum("ibhp,jbhp->bhij", residual, inputs, precision=QUADRATIC)
    grad_b = jnp.einsum("bhij,ibhn->jbhn", pair, c_full, precision=QUADRATIC)
    grad_b = grad_b + to_end[..., None] * jnp.einsum(
        "jbhp,bhnp->jbhn", inputs, adjoint_in, precision=HIGH
    )
    grad_c = jnp.einsum("bhij,jbhn->ibhn", pair, b_full, precision=QUADRATIC)
    grad_c = grad_c + from_start[..., None] * jnp.einsum(
        "ibhp,bhpn->ibhn", residual, state_in, precision=HIGH
    )
    return (grad_x.astype(jnp.bfloat16), grad_b.astype(jnp.bfloat16), grad_c.astype(jnp.bfloat16))


def solution(mesh):
    teach_n, seq_n = mesh.devices.shape
    n_y = FAM
    n_z = teach_n // n_y
    assert n_z == seq_n
    split = Mesh(mesh.devices.reshape(n_z, n_y, seq_n), ("tz", "ty", "seq"))
    placed = (
        P(TEACH, None, "seq"),
        P(TEACH, "seq", None),
        P(),
        P("seq", None, TEACH, None),
        P("seq", None, TEACH, None),
        P("seq", None, TEACH, None),
        P("seq", None, TEACH),
        P("seq", None),
        P(TEACH),
        P(TEACH),
    )
    return jax.shard_map(
        per_device,
        mesh=split,
        in_specs=placed,
        out_specs=(
            P("seq", None, TEACH, None),
            P("seq", None, TEACH, None),
            P("seq", None, TEACH, None),
        ),
        check_vma=False,
    )
```

```python
import jax
import jax.numpy as jnp
from jax import lax
from jax.sharding import Mesh
from jax.sharding import PartitionSpec as P

TD = 5120
P_SIZE = 64
FAM = 8
CAP = 32


EPS = 1e-06
HIGH = lax.Precision.HIGHEST
QUADRATIC = lax.Precision.HIGH
TEACH = ("tz", "ty")


def family_slots(fam_block):
    onehot = (fam_block[..., None] == jnp.arange(FAM, dtype=jnp.int32)[None, None, :]).astype(
        jnp.int32
    )
    before = jnp.cumsum(onehot, axis=1) - onehot
    return jnp.sum(before * onehot, axis=2)


def decay_matrix(log_sums, counts):
    places = jnp.arange(log_sums.shape[0])
    lower = places[:, None] >= places[None, :]
    same_doc = counts.T[:, :, None] == counts.T[:, None, :]
    keep_mask = (lower[None] & same_doc)[:, None]
    sums = log_sums.transpose(1, 2, 0)
    gaps = sums[:, :, :, None] - sums[:, :, None, :]
    return jnp.where(keep_mask, jnp.exp(jnp.where(keep_mask, gaps, 0.0)), 0.0)


def chain_weights(through_all, place, backward):
    count = through_all.shape[0]
    blocks = jnp.arange(count)
    s2 = blocks[:, None]
    s3 = blocks[None, :]
    if backward:
        used = (s3 > place) & (s3 < s2)
        live = blocks > place
    else:
        used = (s3 > s2) & (s3 < place)
        live = blocks < place
    factors = jnp.where(used[:, :, None, None], through_all[None], 1.0)
    weights = jnp.prod(factors, axis=1)
    return jnp.where(live[:, None, None], weights, 0.0)


def combine(weights, local_all):
    return jnp.sum(weights[:, :, :, None, None] * local_all.astype(jnp.float32), axis=0)


def ring_gather(x, axis):
    count = lax.axis_size(axis)
    ahead = [(i, (i + 1) % count) for i in range(count)]
    behind = [(i, (i - 1) % count) for i in range(count)]
    later = [None] * count
    later[0] = x
    cw = x
    ccw = x
    for hop in range(1, count // 2 + 1):
        cw = lax.ppermute(cw, axis, ahead)
        later[count - hop] = cw
        if hop < count - hop:
            ccw = lax.ppermute(ccw, axis, behind)
            later[hop] = ccw
    rel = jnp.stack(later)
    place = lax.axis_index(axis)
    doubled = jnp.concatenate([rel, rel])
    return lax.dynamic_slice_in_dim(doubled, (count - place) % count, count)


def per_device(
    teacher_in, teacher_proj, family, x_in, b_in, c_in, step_size, doc_start, a_rate, skip_gain
):
    n_z = lax.axis_size("tz")
    n_y = lax.axis_size("ty")
    seq_n = lax.axis_size("seq")
    teach_n = n_z * n_y
    heads_all = teach_n * x_in.shape[2]
    block_pos = teacher_in.shape[0]
    batch_n = teacher_in.shape[1]
    feat_width = teacher_in.shape[2]
    block_rows = block_pos * batch_n
    source = lax.axis_index("tz") * n_y + lax.axis_index("ty")
    fam_all = family.reshape(family.shape[0] * family.shape[1])

    own_rows = teacher_in.reshape(block_rows, feat_width)
    own_fam = lax.dynamic_slice_in_dim(fam_all, source * block_rows, block_rows)
    slot_ids = family_slots(own_fam.reshape(1, block_rows))[0]
    dest_cols = own_fam * CAP + slot_ids
    select = (dest_cols[:, None] == jnp.arange(FAM * CAP, dtype=jnp.int32)[None, :]).astype(
        jnp.bfloat16
    )
    packed = jnp.dot(select.T, own_rows, preferred_element_type=jnp.float32).astype(jnp.bfloat16)
    packed = packed.reshape(FAM, CAP, feat_width)
    by_family = lax.all_to_all(packed, "ty", split_axis=0, concat_axis=0, tiled=True)
    received = ring_gather(by_family, "tz")
    x_full = x_in.astype(jnp.float32)
    b_full = b_in.astype(jnp.float32)
    c_full = c_in.astype(jnp.float32)
    log_sums = jnp.cumsum(-step_size * a_rate[None, None, :], axis=0)
    counts = jnp.cumsum(doc_start, axis=0)
    same_end = (counts == counts[-1][None, :]).astype(jnp.float32)
    to_end = jnp.exp(log_sums[-1][None] - log_sums) * same_end[:, :, None]
    from_start = jnp.exp(log_sums) * (counts == 0).astype(jnp.float32)[:, :, None]
    through = jnp.exp(log_sums[-1]) * (counts[-1] == 0).astype(jnp.float32)[:, None]
    inputs = step_size[..., None] * x_full
    local_state = jnp.einsum("jbh,jbhp,jbhn->bhpn", to_end, inputs, b_full, precision=HIGH)
    place = lax.axis_index("seq")
    through_hi = through.astype(jnp.bfloat16)
    through_lo = (through - through_hi.astype(jnp.float32)).astype(jnp.bfloat16)
    edge = local_state.shape[-1]
    packed_state = jnp.concatenate(
        [
            local_state.astype(jnp.bfloat16),
            jnp.broadcast_to(through_hi[:, :, None, None], through.shape + (1, edge)),
            jnp.broadcast_to(through_lo[:, :, None, None], through.shape + (1, edge)),
        ],
        axis=2,
    )
    gathered = lax.all_to_all(
        jnp.broadcast_to(packed_state[None], (seq_n,) + packed_state.shape),
        "seq",
        split_axis=0,
        concat_axis=0,
        tiled=True,
    )
    rows = local_state.shape[2]
    through_all = gathered[:, :, :, rows, 0].astype(jnp.float32) + gathered[
        :, :, :, rows + 1, 0
    ].astype(jnp.float32)
    slots_all = n_z * n_y * CAP
    received = received.reshape(slots_all, feat_width)
    weights = teacher_proj[0]
    partial_value = jnp.dot(received, weights, preferred_element_type=jnp.float32)
    sq_sums = jnp.sum(jnp.square(received.astype(jnp.float32)), axis=1)
    width = partial_value.shape[-1]
    group = n_y * CAP
    partial_value = partial_value.reshape(n_z, group, width)
    sq_all = sq_sums.reshape(n_z, group)
    sq_hi = sq_all.astype(jnp.bfloat16)
    sq_lo = (sq_all - sq_hi.astype(jnp.float32)).astype(jnp.bfloat16)
    sq_row = jnp.concatenate([sq_hi, sq_lo], axis=1)[:, None, :]
    outbound = jnp.concatenate([partial_value.astype(jnp.bfloat16), sq_row], axis=1)
    inbound = lax.all_to_all(outbound, "seq", split_axis=0, concat_axis=0, tiled=True)
    summed = jnp.sum(inbound.astype(jnp.float32), axis=0)
    sq_total = summed[group, :group] + summed[group, group : 2 * group]
    row_scale = lax.rsqrt(sq_total / TD + EPS)
    scaled = (summed[:group] * row_scale[:, None]).astype(jnp.bfloat16)
    scaled = scaled.reshape(group, heads_all, -1)
    cols = scaled.shape[-1]
    outgoing = scaled.transpose(1, 0, 2)
    arrived = lax.all_to_all(outgoing, TEACH, split_axis=0, concat_axis=0, tiled=True)
    arrived = arrived.reshape(n_z, n_y, n_y * CAP, cols)
    table = arrived.reshape(n_z, n_y * n_y * CAP, cols)

    shard_rows = n_y * block_rows
    shard_fam = lax.dynamic_slice_in_dim(
        fam_all, lax.axis_index("seq") * shard_rows, shard_rows
    ).reshape(n_y, block_rows)
    shard_slots = family_slots(shard_fam)
    sources = jnp.arange(n_y, dtype=jnp.int32)[:, None]
    row_index = ((shard_fam * n_y + sources) * CAP + shard_slots).reshape(shard_rows)
    chooser = (row_index[:, None] == jnp.arange(table.shape[1], dtype=jnp.int32)[None, :]).astype(
        jnp.bfloat16
    )
    picked = jnp.einsum("rq,jqc->rjc", chooser, table, preferred_element_type=jnp.float32)
    target = picked.reshape(n_y * block_pos, batch_n, 1, P_SIZE)

    state_in = combine(chain_weights(through_all, place, False), gathered[:, :, :, :rows])
    decay_mat = decay_matrix(log_sums, counts)
    scores = jnp.einsum("ibhn,jbhn->bhij", c_in, b_in, preferred_element_type=jnp.float32)
    mixing = decay_mat * scores
    output = jnp.einsum("bhij,jbhp->ibhp", mixing, inputs, precision=QUADRATIC)
    output = output + from_start[..., None] * jnp.einsum(
        "ibhn,bhpn->ibhp", c_full, state_in, precision=HIGH
    )
    output = output + skip_gain[None, None, :, None] * x_full
    residual = output - target.astype(jnp.float32)
    local_adjoint = jnp.einsum("ibh,ibhn,ibhp->bhnp", from_start, c_full, residual, precision=HIGH)
    adjoint_all = lax.all_to_all(
        jnp.broadcast_to(local_adjoint.astype(jnp.bfloat16)[None], (seq_n,) + local_adjoint.shape),
        "seq",
        split_axis=0,
        concat_axis=0,
        tiled=True,
    )
    adjoint_in = combine(chain_weights(through_all, place, True), adjoint_all)
    grad_u = jnp.einsum("bhij,ibhp->jbhp", mixing, residual, precision=QUADRATIC)
    grad_u = grad_u + to_end[..., None] * jnp.einsum(
        "jbhn,bhnp->jbhp", b_full, adjoint_in, precision=HIGH
    )
    grad_x = step_size[..., None] * grad_u + skip_gain[None, None, :, None] * residual
    pair = decay_mat * jnp.einsum("ibhp,jbhp->bhij", residual, inputs, precision=QUADRATIC)
    grad_b = jnp.einsum("bhij,ibhn->jbhn", pair, c_full, precision=QUADRATIC)
    grad_b = grad_b + to_end[..., None] * jnp.einsum(
        "jbhp,bhnp->jbhn", inputs, adjoint_in, precision=HIGH
    )
    grad_c = jnp.einsum("bhij,jbhn->ibhn", pair, b_full, precision=QUADRATIC)
    grad_c = grad_c + from_start[..., None] * jnp.einsum(
        "ibhp,bhpn->ibhn", residual, state_in, precision=HIGH
    )
    return (grad_x.astype(jnp.bfloat16), grad_b.astype(jnp.bfloat16), grad_c.astype(jnp.bfloat16))


def solution(mesh):
    teach_n, seq_n = mesh.devices.shape
    n_y = FAM
    n_z = teach_n // n_y
    assert n_z == seq_n
    split = Mesh(mesh.devices.reshape(n_z, n_y, seq_n), ("tz", "ty", "seq"))
    placed = (
        P(TEACH, None, "seq"),
        P(TEACH, "seq", None),
        P(),
        P("seq", None, TEACH, None),
        P("seq", None, TEACH, None),
        P("seq", None, TEACH, None),
        P("seq", None, TEACH),
        P("seq", None),
        P(TEACH),
        P(TEACH),
    )
    return jax.shard_map(
        per_device,
        mesh=split,
        in_specs=placed,
        out_specs=(
            P("seq", None, TEACH, None),
            P("seq", None, TEACH, None),
            P("seq", None, TEACH, None),
        ),
        check_vma=False,
    )
```

```python
import jax
import jax.numpy as jnp
from jax import lax
from jax.sharding import Mesh
from jax.sharding import PartitionSpec as P

TD = 5120
P_SIZE = 64
FAM = 8
CAP = 32


EPS = 1e-06
HIGH = lax.Precision.HIGHEST
QUADRATIC = lax.Precision.HIGH
TEACH = ("tz", "ty")


def family_slots(fam_block):
    onehot = (fam_block[..., None] == jnp.arange(FAM, dtype=jnp.int32)[None, None, :]).astype(
        jnp.int32
    )
    before = jnp.cumsum(onehot, axis=1) - onehot
    return jnp.sum(before * onehot, axis=2)


def decay_matrix(log_sums, counts):
    places = jnp.arange(log_sums.shape[0])
    lower = places[:, None] >= places[None, :]
    same_doc = counts.T[:, :, None] == counts.T[:, None, :]
    keep_mask = (lower[None] & same_doc)[:, None]
    sums = log_sums.transpose(1, 2, 0)
    gaps = sums[:, :, :, None] - sums[:, :, None, :]
    return jnp.where(keep_mask, jnp.exp(jnp.where(keep_mask, gaps, 0.0)), 0.0)


def chain_weights(through_all, place, backward):
    count = through_all.shape[0]
    blocks = jnp.arange(count)
    s2 = blocks[:, None]
    s3 = blocks[None, :]
    if backward:
        used = (s3 > place) & (s3 < s2)
        live = blocks > place
    else:
        used = (s3 > s2) & (s3 < place)
        live = blocks < place
    factors = jnp.where(used[:, :, None, None], through_all[None], 1.0)
    weights = jnp.prod(factors, axis=1)
    return jnp.where(live[:, None, None], weights, 0.0)


def combine(weights, local_all):
    return jnp.sum(weights[:, :, :, None, None] * local_all.astype(jnp.float32), axis=0)


def ring_gather(x, axis):
    count = lax.axis_size(axis)
    ahead = [(i, (i + 1) % count) for i in range(count)]
    behind = [(i, (i - 1) % count) for i in range(count)]
    later = [None] * count
    later[0] = x
    cw = x
    ccw = x
    for hop in range(1, count // 2 + 1):
        cw = lax.ppermute(cw, axis, ahead)
        later[count - hop] = cw
        if hop < count - hop:
            ccw = lax.ppermute(ccw, axis, behind)
            later[hop] = ccw
    rel = jnp.stack(later)
    place = lax.axis_index(axis)
    doubled = jnp.concatenate([rel, rel])
    return lax.dynamic_slice_in_dim(doubled, (count - place) % count, count)


def per_device(
    teacher_in, teacher_proj, family, x_in, b_in, c_in, step_size, doc_start, a_rate, skip_gain
):
    n_z = lax.axis_size("tz")
    n_y = lax.axis_size("ty")
    seq_n = lax.axis_size("seq")
    teach_n = n_z * n_y
    heads_all = teach_n * x_in.shape[2]
    block_pos = teacher_in.shape[0]
    batch_n = teacher_in.shape[1]
    feat_width = teacher_in.shape[2]
    block_rows = block_pos * batch_n
    source = lax.axis_index("tz") * n_y + lax.axis_index("ty")
    fam_all = family.reshape(family.shape[0] * family.shape[1])

    own_rows = teacher_in.reshape(block_rows, feat_width)
    own_fam = lax.dynamic_slice_in_dim(fam_all, source * block_rows, block_rows)
    slot_ids = family_slots(own_fam.reshape(1, block_rows))[0]
    dest_cols = own_fam * CAP + slot_ids
    select = (dest_cols[:, None] == jnp.arange(FAM * CAP, dtype=jnp.int32)[None, :]).astype(
        jnp.bfloat16
    )
    packed = jnp.dot(select.T, own_rows, preferred_element_type=jnp.float32).astype(jnp.bfloat16)
    packed = packed.reshape(FAM, CAP, feat_width)
    by_family = lax.all_to_all(packed, "ty", split_axis=0, concat_axis=0, tiled=True)
    received = ring_gather(by_family, "tz")
    x_full = x_in.astype(jnp.float32)
    b_full = b_in.astype(jnp.float32)
    c_full = c_in.astype(jnp.float32)
    log_sums = jnp.cumsum(-step_size * a_rate[None, None, :], axis=0)
    counts = jnp.cumsum(doc_start, axis=0)
    same_end = (counts == counts[-1][None, :]).astype(jnp.float32)
    to_end = jnp.exp(log_sums[-1][None] - log_sums) * same_end[:, :, None]
    from_start = jnp.exp(log_sums) * (counts == 0).astype(jnp.float32)[:, :, None]
    through = jnp.exp(log_sums[-1]) * (counts[-1] == 0).astype(jnp.float32)[:, None]
    inputs = step_size[..., None] * x_full
    local_state = jnp.einsum("jbh,jbhp,jbhn->bhpn", to_end, inputs, b_full, precision=HIGH)
    place = lax.axis_index("seq")
    through_hi = through.astype(jnp.bfloat16)
    through_lo = (through - through_hi.astype(jnp.float32)).astype(jnp.bfloat16)
    edge = local_state.shape[-1]
    packed_state = jnp.concatenate(
        [
            local_state.astype(jnp.bfloat16),
            jnp.broadcast_to(through_hi[:, :, None, None], through.shape + (1, edge)),
            jnp.broadcast_to(through_lo[:, :, None, None], through.shape + (1, edge)),
        ],
        axis=2,
    )
    slots_all = n_z * n_y * CAP
    received = received.reshape(slots_all, feat_width)
    weights = teacher_proj[0]
    partial_value = jnp.dot(received, weights, preferred_element_type=jnp.float32)
    sq_sums = jnp.sum(jnp.square(received.astype(jnp.float32)), axis=1)
    width = partial_value.shape[-1]
    group = n_y * CAP
    partial_value = partial_value.reshape(n_z, group, width)
    sq_all = sq_sums.reshape(n_z, group)
    sq_hi = sq_all.astype(jnp.bfloat16)
    sq_lo = (sq_all - sq_hi.astype(jnp.float32)).astype(jnp.bfloat16)
    sq_row = jnp.concatenate([sq_hi, sq_lo], axis=1)[:, None, :]
    state_rows = jnp.broadcast_to(
        packed_state.reshape(1, -1, width), (n_z, packed_state.size // width, width)
    )
    outbound = jnp.concatenate([partial_value.astype(jnp.bfloat16), sq_row, state_rows], axis=1)
    inbound = lax.all_to_all(outbound, "seq", split_axis=0, concat_axis=0, tiled=True)
    summed = jnp.sum(inbound[:, : group + 1].astype(jnp.float32), axis=0)
    gathered = inbound[:, group + 1 :].reshape((seq_n,) + packed_state.shape)
    rows = local_state.shape[2]
    through_all = gathered[:, :, :, rows, 0].astype(jnp.float32) + gathered[
        :, :, :, rows + 1, 0
    ].astype(jnp.float32)
    sq_total = summed[group, :group] + summed[group, group : 2 * group]
    row_scale = lax.rsqrt(sq_total / TD + EPS)
    scaled = (summed[:group] * row_scale[:, None]).astype(jnp.bfloat16)
    scaled = scaled.reshape(group, heads_all, -1)
    cols = scaled.shape[-1]
    outgoing = scaled.transpose(1, 0, 2)
    arrived = lax.all_to_all(outgoing, TEACH, split_axis=0, concat_axis=0, tiled=True)
    arrived = arrived.reshape(n_z, n_y, n_y * CAP, cols)
    table = arrived.reshape(n_z, n_y * n_y * CAP, cols)

    shard_rows = n_y * block_rows
    shard_fam = lax.dynamic_slice_in_dim(
        fam_all, lax.axis_index("seq") * shard_rows, shard_rows
    ).reshape(n_y, block_rows)
    shard_slots = family_slots(shard_fam)
    sources = jnp.arange(n_y, dtype=jnp.int32)[:, None]
    row_index = ((shard_fam * n_y + sources) * CAP + shard_slots).reshape(shard_rows)
    chooser = (row_index[:, None] == jnp.arange(table.shape[1], dtype=jnp.int32)[None, :]).astype(
        jnp.bfloat16
    )
    picked = jnp.einsum("rq,jqc->rjc", chooser, table, preferred_element_type=jnp.float32)
    target = picked.reshape(n_y * block_pos, batch_n, 1, P_SIZE)

    state_in = combine(chain_weights(through_all, place, False), gathered[:, :, :, :rows])
    decay_mat = decay_matrix(log_sums, counts)
    scores = jnp.einsum("ibhn,jbhn->bhij", c_in, b_in, preferred_element_type=jnp.float32)
    mixing = decay_mat * scores
    output = jnp.einsum("bhij,jbhp->ibhp", mixing, inputs, precision=QUADRATIC)
    output = output + from_start[..., None] * jnp.einsum(
        "ibhn,bhpn->ibhp", c_full, state_in, precision=HIGH
    )
    output = output + skip_gain[None, None, :, None] * x_full
    residual = output - target.astype(jnp.float32)
    local_adjoint = jnp.einsum("ibh,ibhn,ibhp->bhnp", from_start, c_full, residual, precision=HIGH)
    adjoint_all = lax.all_to_all(
        jnp.broadcast_to(local_adjoint.astype(jnp.bfloat16)[None], (seq_n,) + local_adjoint.shape),
        "seq",
        split_axis=0,
        concat_axis=0,
        tiled=True,
    )
    adjoint_in = combine(chain_weights(through_all, place, True), adjoint_all)
    grad_u = jnp.einsum("bhij,ibhp->jbhp", mixing, residual, precision=QUADRATIC)
    grad_u = grad_u + to_end[..., None] * jnp.einsum(
        "jbhn,bhnp->jbhp", b_full, adjoint_in, precision=HIGH
    )
    grad_x = step_size[..., None] * grad_u + skip_gain[None, None, :, None] * residual
    pair = decay_mat * jnp.einsum("ibhp,jbhp->bhij", residual, inputs, precision=QUADRATIC)
    grad_b = jnp.einsum("bhij,ibhn->jbhn", pair, c_full, precision=QUADRATIC)
    grad_b = grad_b + to_end[..., None] * jnp.einsum(
        "jbhp,bhnp->jbhn", inputs, adjoint_in, precision=HIGH
    )
    grad_c = jnp.einsum("bhij,jbhn->ibhn", pair, b_full, precision=QUADRATIC)
    grad_c = grad_c + from_start[..., None] * jnp.einsum(
        "ibhp,bhpn->ibhn", residual, state_in, precision=HIGH
    )
    return (grad_x.astype(jnp.bfloat16), grad_b.astype(jnp.bfloat16), grad_c.astype(jnp.bfloat16))


def solution(mesh):
    teach_n, seq_n = mesh.devices.shape
    n_y = FAM
    n_z = teach_n // n_y
    assert n_z == seq_n
    split = Mesh(mesh.devices.reshape(n_z, n_y, seq_n), ("tz", "ty", "seq"))
    placed = (
        P(TEACH, None, "seq"),
        P(TEACH, "seq", None),
        P(),
        P("seq", None, TEACH, None),
        P("seq", None, TEACH, None),
        P("seq", None, TEACH, None),
        P("seq", None, TEACH),
        P("seq", None),
        P(TEACH),
        P(TEACH),
    )
    return jax.shard_map(
        per_device,
        mesh=split,
        in_specs=placed,
        out_specs=(
            P("seq", None, TEACH, None),
            P("seq", None, TEACH, None),
            P("seq", None, TEACH, None),
        ),
        check_vma=False,
    )
```

```python
import jax
import jax.numpy as jnp
from jax import lax
from jax.sharding import Mesh
from jax.sharding import PartitionSpec as P

TD = 5120
P_SIZE = 64
FAM = 8
CAP = 32


EPS = 1e-06
HIGH = lax.Precision.HIGHEST
QUADRATIC = lax.Precision.HIGH
TEACH = ("tz", "ty")


def family_slots(fam_block):
    onehot = (fam_block[..., None] == jnp.arange(FAM, dtype=jnp.int32)[None, None, :]).astype(
        jnp.int32
    )
    before = jnp.cumsum(onehot, axis=1) - onehot
    return jnp.sum(before * onehot, axis=2)


def decay_matrix(log_sums, counts):
    places = jnp.arange(log_sums.shape[0])
    lower = places[:, None] >= places[None, :]
    same_doc = counts.T[:, :, None] == counts.T[:, None, :]
    keep_mask = (lower[None] & same_doc)[:, None]
    sums = log_sums.transpose(1, 2, 0)
    gaps = sums[:, :, :, None] - sums[:, :, None, :]
    return jnp.where(keep_mask, jnp.exp(jnp.where(keep_mask, gaps, 0.0)), 0.0)


def chain_weights(through_all, place, backward):
    count = through_all.shape[0]
    blocks = jnp.arange(count)
    s2 = blocks[:, None]
    s3 = blocks[None, :]
    if backward:
        used = (s3 > place) & (s3 < s2)
        live = blocks > place
    else:
        used = (s3 > s2) & (s3 < place)
        live = blocks < place
    factors = jnp.where(used[:, :, None, None], through_all[None], 1.0)
    weights = jnp.prod(factors, axis=1)
    return jnp.where(live[:, None, None], weights, 0.0)


def combine(weights, local_all):
    return jnp.sum(weights[:, :, :, None, None] * local_all.astype(jnp.float32), axis=0)


def ring_gather(x, axis):
    count = lax.axis_size(axis)
    ahead = [(i, (i + 1) % count) for i in range(count)]
    behind = [(i, (i - 1) % count) for i in range(count)]
    later = [None] * count
    later[0] = x
    cw = x
    ccw = x
    for hop in range(1, count // 2 + 1):
        cw = lax.ppermute(cw, axis, ahead)
        later[count - hop] = cw
        if hop < count - hop:
            ccw = lax.ppermute(ccw, axis, behind)
            later[hop] = ccw
    rel = jnp.stack(later)
    place = lax.axis_index(axis)
    doubled = jnp.concatenate([rel, rel])
    return lax.dynamic_slice_in_dim(doubled, (count - place) % count, count)


def per_device(
    teacher_in, teacher_proj, family, x_in, b_in, c_in, step_size, doc_start, a_rate, skip_gain
):
    n_z = lax.axis_size("tz")
    n_y = lax.axis_size("ty")
    seq_n = lax.axis_size("seq")
    teach_n = n_z * n_y
    heads_all = teach_n * x_in.shape[2]
    block_pos = teacher_in.shape[0]
    batch_n = teacher_in.shape[1]
    feat_width = teacher_in.shape[2]
    block_rows = block_pos * batch_n
    source = lax.axis_index("tz") * n_y + lax.axis_index("ty")
    fam_all = family.reshape(family.shape[0] * family.shape[1])

    own_rows = teacher_in.reshape(block_rows, feat_width)
    own_fam = lax.dynamic_slice_in_dim(fam_all, source * block_rows, block_rows)
    slot_ids = family_slots(own_fam.reshape(1, block_rows))[0]
    dest_cols = own_fam * CAP + slot_ids
    select = (dest_cols[:, None] == jnp.arange(FAM * CAP, dtype=jnp.int32)[None, :]).astype(
        jnp.bfloat16
    )
    packed = jnp.dot(select.T, own_rows, preferred_element_type=jnp.float32).astype(jnp.bfloat16)
    packed = packed.reshape(FAM, CAP, feat_width)
    by_family = lax.all_to_all(packed, "ty", split_axis=0, concat_axis=0, tiled=True)
    received = ring_gather(by_family, "tz")
    x_full = x_in.astype(jnp.float32)
    b_full = b_in.astype(jnp.float32)
    c_full = c_in.astype(jnp.float32)
    log_sums = jnp.cumsum(-step_size * a_rate[None, None, :], axis=0)
    counts = jnp.cumsum(doc_start, axis=0)
    same_end = (counts == counts[-1][None, :]).astype(jnp.float32)
    to_end = jnp.exp(log_sums[-1][None] - log_sums) * same_end[:, :, None]
    from_start = jnp.exp(log_sums) * (counts == 0).astype(jnp.float32)[:, :, None]
    through = jnp.exp(log_sums[-1]) * (counts[-1] == 0).astype(jnp.float32)[:, None]
    inputs = step_size[..., None] * x_full
    local_state = jnp.einsum("jbh,jbhp,jbhn->bhpn", to_end, inputs, b_full, precision=HIGH)
    place = lax.axis_index("seq")
    through_hi = through.astype(jnp.bfloat16)
    through_lo = (through - through_hi.astype(jnp.float32)).astype(jnp.bfloat16)
    edge = local_state.shape[-1]
    packed_state = jnp.concatenate(
        [
            local_state.astype(jnp.bfloat16),
            jnp.broadcast_to(through_hi[:, :, None, None], through.shape + (1, edge)),
            jnp.broadcast_to(through_lo[:, :, None, None], through.shape + (1, edge)),
        ],
        axis=2,
    )
    slots_all = n_z * n_y * CAP
    received = received.reshape(slots_all, feat_width)
    weights = teacher_proj[0]
    partial_value = jnp.dot(received, weights, preferred_element_type=jnp.float32)
    sq_sums = jnp.sum(jnp.square(received.astype(jnp.float32)), axis=1)
    width = partial_value.shape[-1]
    group = n_y * CAP
    partial_value = partial_value.reshape(n_z, group, width)
    sq_all = sq_sums.reshape(n_z, group)
    sq_hi = sq_all.astype(jnp.bfloat16)
    sq_lo = (sq_all - sq_hi.astype(jnp.float32)).astype(jnp.bfloat16)
    sq_row = jnp.concatenate([sq_hi, sq_lo], axis=1)[:, None, :]
    state_rows = jnp.broadcast_to(
        packed_state.reshape(1, -1, width), (n_z, packed_state.size // width, width)
    )
    outbound = jnp.concatenate([partial_value.astype(jnp.bfloat16), sq_row, state_rows], axis=1)
    inbound = lax.all_to_all(outbound, "seq", split_axis=0, concat_axis=0, tiled=True)
    summed = jnp.sum(inbound[:, : group + 1].astype(jnp.float32), axis=0)
    gathered = inbound[:, group + 1 :].reshape((seq_n,) + packed_state.shape)
    rows = local_state.shape[2]
    through_all = gathered[:, :, :, rows, 0].astype(jnp.float32) + gathered[
        :, :, :, rows + 1, 0
    ].astype(jnp.float32)
    sq_total = summed[group, :group] + summed[group, group : 2 * group]
    row_scale = lax.rsqrt(sq_total / TD + EPS)
    scaled = (summed[:group] * row_scale[:, None]).astype(jnp.bfloat16)
    scaled = scaled.reshape(group, heads_all, -1)
    cols = scaled.shape[-1]
    outgoing = scaled.transpose(1, 2, 0)
    arrived = lax.all_to_all(outgoing, TEACH, split_axis=0, concat_axis=0, tiled=True)
    table = arrived.reshape(n_z, n_y, cols, n_y * CAP)

    shard_rows = n_y * block_rows
    shard_fam = lax.dynamic_slice_in_dim(
        fam_all, lax.axis_index("seq") * shard_rows, shard_rows
    ).reshape(n_y, block_rows)
    shard_slots = family_slots(shard_fam)
    sources = jnp.arange(n_y, dtype=jnp.int32)[:, None]
    row_index = ((shard_fam * n_y + sources) * CAP + shard_slots).reshape(shard_rows)
    chooser = (row_index[:, None] == jnp.arange(n_y * n_y * CAP, dtype=jnp.int32)[None, :]).astype(
        jnp.bfloat16
    )
    chooser = chooser.reshape(shard_rows, n_y, n_y * CAP)
    picked = jnp.einsum("rfq,jfcq->rjc", chooser, table, preferred_element_type=jnp.float32)
    target = picked.reshape(n_y * block_pos, batch_n, 1, P_SIZE)

    state_in = combine(chain_weights(through_all, place, False), gathered[:, :, :, :rows])
    decay_mat = decay_matrix(log_sums, counts)
    scores = jnp.einsum("ibhn,jbhn->bhij", c_in, b_in, preferred_element_type=jnp.float32)
    mixing = decay_mat * scores
    output = jnp.einsum("bhij,jbhp->ibhp", mixing, inputs, precision=QUADRATIC)
    output = output + from_start[..., None] * jnp.einsum(
        "ibhn,bhpn->ibhp", c_full, state_in, precision=HIGH
    )
    output = output + skip_gain[None, None, :, None] * x_full
    residual = output - target.astype(jnp.float32)
    local_adjoint = jnp.einsum("ibh,ibhn,ibhp->bhnp", from_start, c_full, residual, precision=HIGH)
    adjoint_all = lax.all_to_all(
        jnp.broadcast_to(local_adjoint.astype(jnp.bfloat16)[None], (seq_n,) + local_adjoint.shape),
        "seq",
        split_axis=0,
        concat_axis=0,
        tiled=True,
    )
    adjoint_in = combine(chain_weights(through_all, place, True), adjoint_all)
    grad_u = jnp.einsum("bhij,ibhp->jbhp", mixing, residual, precision=QUADRATIC)
    grad_u = grad_u + to_end[..., None] * jnp.einsum(
        "jbhn,bhnp->jbhp", b_full, adjoint_in, precision=HIGH
    )
    grad_x = step_size[..., None] * grad_u + skip_gain[None, None, :, None] * residual
    pair = decay_mat * jnp.einsum("ibhp,jbhp->bhij", residual, inputs, precision=QUADRATIC)
    grad_b = jnp.einsum("bhij,ibhn->jbhn", pair, c_full, precision=QUADRATIC)
    grad_b = grad_b + to_end[..., None] * jnp.einsum(
        "jbhp,bhnp->jbhn", inputs, adjoint_in, precision=HIGH
    )
    grad_c = jnp.einsum("bhij,jbhn->ibhn", pair, b_full, precision=QUADRATIC)
    grad_c = grad_c + from_start[..., None] * jnp.einsum(
        "ibhp,bhpn->ibhn", residual, state_in, precision=HIGH
    )
    return (grad_x.astype(jnp.bfloat16), grad_b.astype(jnp.bfloat16), grad_c.astype(jnp.bfloat16))


def solution(mesh):
    teach_n, seq_n = mesh.devices.shape
    n_y = FAM
    n_z = teach_n // n_y
    assert n_z == seq_n
    split = Mesh(mesh.devices.reshape(n_z, n_y, seq_n), ("tz", "ty", "seq"))
    placed = (
        P(TEACH, None, "seq"),
        P(TEACH, "seq", None),
        P(),
        P("seq", None, TEACH, None),
        P("seq", None, TEACH, None),
        P("seq", None, TEACH, None),
        P("seq", None, TEACH),
        P("seq", None),
        P(TEACH),
        P(TEACH),
    )
    return jax.shard_map(
        per_device,
        mesh=split,
        in_specs=placed,
        out_specs=(
            P("seq", None, TEACH, None),
            P("seq", None, TEACH, None),
            P("seq", None, TEACH, None),
        ),
        check_vma=False,
    )
```

```python
import jax
import jax.numpy as jnp
from jax import lax
from jax.sharding import Mesh
from jax.sharding import PartitionSpec as P

TD = 5120
P_SIZE = 64
FAM = 8
CAP = 32


EPS = 1e-06
HIGH = lax.Precision.HIGHEST
QUADRATIC = lax.Precision.HIGH
TEACH = ("tz", "ty")


def family_slots(fam_block):
    onehot = (fam_block[..., None] == jnp.arange(FAM, dtype=jnp.int32)[None, None, :]).astype(
        jnp.int32
    )
    before = jnp.cumsum(onehot, axis=1) - onehot
    return jnp.sum(before * onehot, axis=2)


def decay_matrix(log_sums, counts):
    places = jnp.arange(log_sums.shape[0])
    lower = places[:, None] >= places[None, :]
    same_doc = counts.T[:, :, None] == counts.T[:, None, :]
    keep_mask = (lower[None] & same_doc)[:, None]
    sums = log_sums.transpose(1, 2, 0)
    gaps = sums[:, :, :, None] - sums[:, :, None, :]
    return jnp.where(keep_mask, jnp.exp(jnp.where(keep_mask, gaps, 0.0)), 0.0)


def chain_weights(through_all, place, backward):
    count = through_all.shape[0]
    blocks = jnp.arange(count)
    s2 = blocks[:, None]
    s3 = blocks[None, :]
    if backward:
        used = (s3 > place) & (s3 < s2)
        live = blocks > place
    else:
        used = (s3 > s2) & (s3 < place)
        live = blocks < place
    factors = jnp.where(used[:, :, None, None], through_all[None], 1.0)
    weights = jnp.prod(factors, axis=1)
    return jnp.where(live[:, None, None], weights, 0.0)


def combine(weights, local_all):
    return jnp.sum(weights[:, :, :, None, None] * local_all.astype(jnp.float32), axis=0)


def ring_gather(x, axis):
    count = lax.axis_size(axis)
    ahead = [(i, (i + 1) % count) for i in range(count)]
    behind = [(i, (i - 1) % count) for i in range(count)]
    later = [None] * count
    later[0] = x
    cw = x
    ccw = x
    for hop in range(1, count // 2 + 1):
        cw = lax.ppermute(cw, axis, ahead)
        later[count - hop] = cw
        if hop < count - hop:
            ccw = lax.ppermute(ccw, axis, behind)
            later[hop] = ccw
    rel = jnp.stack(later)
    place = lax.axis_index(axis)
    doubled = jnp.concatenate([rel, rel])
    return lax.dynamic_slice_in_dim(doubled, (count - place) % count, count)


def per_device(
    teacher_in, teacher_proj, family, x_in, b_in, c_in, step_size, doc_start, a_rate, skip_gain
):
    n_z = lax.axis_size("tz")
    n_y = lax.axis_size("ty")
    seq_n = lax.axis_size("seq")
    teach_n = n_z * n_y
    heads_all = teach_n * x_in.shape[2]
    block_pos = teacher_in.shape[0]
    batch_n = teacher_in.shape[1]
    feat_width = teacher_in.shape[2]
    block_rows = block_pos * batch_n
    source = lax.axis_index("tz") * n_y + lax.axis_index("ty")

    own_rows = teacher_in.reshape(block_rows, feat_width)
    own_fam = lax.dynamic_slice_in_dim(family, source * block_pos, block_pos).reshape(block_rows)
    slot_ids = family_slots(own_fam.reshape(1, block_rows))[0]
    dest_cols = own_fam * CAP + slot_ids
    select = (dest_cols[:, None] == jnp.arange(FAM * CAP, dtype=jnp.int32)[None, :]).astype(
        jnp.bfloat16
    )
    packed = jnp.dot(select.T, own_rows, preferred_element_type=jnp.float32).astype(jnp.bfloat16)
    packed = packed.reshape(FAM, CAP, feat_width)
    by_family = lax.all_to_all(packed, "ty", split_axis=0, concat_axis=0, tiled=True)
    received = ring_gather(by_family, "tz")
    x_full = x_in.astype(jnp.float32)
    b_full = b_in.astype(jnp.float32)
    c_full = c_in.astype(jnp.float32)
    log_sums = jnp.cumsum(-step_size * a_rate[None, None, :], axis=0)
    counts = jnp.cumsum(doc_start, axis=0)
    same_end = (counts == counts[-1][None, :]).astype(jnp.float32)
    to_end = jnp.exp(log_sums[-1][None] - log_sums) * same_end[:, :, None]
    from_start = jnp.exp(log_sums) * (counts == 0).astype(jnp.float32)[:, :, None]
    through = jnp.exp(log_sums[-1]) * (counts[-1] == 0).astype(jnp.float32)[:, None]
    inputs = step_size[..., None] * x_full
    local_state = jnp.einsum("jbh,jbhp,jbhn->bhpn", to_end, inputs, b_full, precision=HIGH)
    place = lax.axis_index("seq")
    through_hi = through.astype(jnp.bfloat16)
    through_lo = (through - through_hi.astype(jnp.float32)).astype(jnp.bfloat16)
    edge = local_state.shape[-1]
    packed_state = jnp.concatenate(
        [
            local_state.astype(jnp.bfloat16),
            jnp.broadcast_to(through_hi[:, :, None, None], through.shape + (1, edge)),
            jnp.broadcast_to(through_lo[:, :, None, None], through.shape + (1, edge)),
        ],
        axis=2,
    )
    slots_all = n_z * n_y * CAP
    received = received.reshape(slots_all, feat_width)
    weights = teacher_proj[0]
    partial_value = jnp.dot(received, weights, preferred_element_type=jnp.float32)
    sq_sums = jnp.sum(jnp.square(received.astype(jnp.float32)), axis=1)
    width = partial_value.shape[-1]
    group = n_y * CAP
    partial_value = partial_value.reshape(n_z, group, width)
    sq_all = sq_sums.reshape(n_z, group)
    sq_hi = sq_all.astype(jnp.bfloat16)
    sq_lo = (sq_all - sq_hi.astype(jnp.float32)).astype(jnp.bfloat16)
    sq_row = jnp.concatenate([sq_hi, sq_lo], axis=1)[:, None, :]
    state_rows = jnp.broadcast_to(
        packed_state.reshape(1, -1, width), (n_z, packed_state.size // width, width)
    )
    outbound = jnp.concatenate([partial_value.astype(jnp.bfloat16), sq_row, state_rows], axis=1)
    inbound = lax.all_to_all(outbound, "seq", split_axis=0, concat_axis=0, tiled=True)
    summed = jnp.sum(inbound[:, : group + 1].astype(jnp.float32), axis=0)
    gathered = inbound[:, group + 1 :].reshape((seq_n,) + packed_state.shape)
    rows = local_state.shape[2]
    through_all = gathered[:, :, :, rows, 0].astype(jnp.float32) + gathered[
        :, :, :, rows + 1, 0
    ].astype(jnp.float32)
    sq_total = summed[group, :group] + summed[group, group : 2 * group]
    row_scale = lax.rsqrt(sq_total / TD + EPS)
    scaled = (summed[:group] * row_scale[:, None]).astype(jnp.bfloat16)
    scaled = scaled.reshape(group, heads_all, -1)
    cols = scaled.shape[-1]
    outgoing = scaled.transpose(1, 2, 0)
    arrived = lax.all_to_all(outgoing, TEACH, split_axis=0, concat_axis=0, tiled=True)
    table = arrived.reshape(n_z, n_y, cols, n_y * CAP)

    shard_rows = n_y * block_rows
    shard_fam = lax.dynamic_slice_in_dim(
        family, lax.axis_index("seq") * (n_y * block_pos), n_y * block_pos
    ).reshape(n_y, block_rows)
    shard_slots = family_slots(shard_fam)
    sources = jnp.arange(n_y, dtype=jnp.int32)[:, None]
    row_index = ((shard_fam * n_y + sources) * CAP + shard_slots).reshape(shard_rows)
    chooser = (row_index[:, None] == jnp.arange(n_y * n_y * CAP, dtype=jnp.int32)[None, :]).astype(
        jnp.bfloat16
    )
    chooser = chooser.reshape(shard_rows, n_y, n_y * CAP)
    picked = jnp.einsum("rfq,jfcq->rjc", chooser, table, preferred_element_type=jnp.float32)
    target = picked.reshape(n_y * block_pos, batch_n, 1, P_SIZE)

    state_in = combine(chain_weights(through_all, place, False), gathered[:, :, :, :rows])
    decay_mat = decay_matrix(log_sums, counts)
    scores = jnp.einsum("ibhn,jbhn->bhij", c_in, b_in, preferred_element_type=jnp.float32)
    mixing = decay_mat * scores
    output = jnp.einsum("bhij,jbhp->ibhp", mixing, inputs, precision=QUADRATIC)
    output = output + from_start[..., None] * jnp.einsum(
        "ibhn,bhpn->ibhp", c_full, state_in, precision=HIGH
    )
    output = output + skip_gain[None, None, :, None] * x_full
    residual = output - target.astype(jnp.float32)
    local_adjoint = jnp.einsum("ibh,ibhn,ibhp->bhnp", from_start, c_full, residual, precision=HIGH)
    adjoint_all = lax.all_to_all(
        jnp.broadcast_to(local_adjoint.astype(jnp.bfloat16)[None], (seq_n,) + local_adjoint.shape),
        "seq",
        split_axis=0,
        concat_axis=0,
        tiled=True,
    )
    adjoint_in = combine(chain_weights(through_all, place, True), adjoint_all)
    grad_u = jnp.einsum("bhij,ibhp->jbhp", mixing, residual, precision=QUADRATIC)
    grad_u = grad_u + to_end[..., None] * jnp.einsum(
        "jbhn,bhnp->jbhp", b_full, adjoint_in, precision=HIGH
    )
    grad_x = step_size[..., None] * grad_u + skip_gain[None, None, :, None] * residual
    pair = decay_mat * jnp.einsum("ibhp,jbhp->bhij", residual, inputs, precision=QUADRATIC)
    grad_b = jnp.einsum("bhij,ibhn->jbhn", pair, c_full, precision=QUADRATIC)
    grad_b = grad_b + to_end[..., None] * jnp.einsum(
        "jbhp,bhnp->jbhn", inputs, adjoint_in, precision=HIGH
    )
    grad_c = jnp.einsum("bhij,jbhn->ibhn", pair, b_full, precision=QUADRATIC)
    grad_c = grad_c + from_start[..., None] * jnp.einsum(
        "ibhp,bhpn->ibhn", residual, state_in, precision=HIGH
    )
    return (grad_x.astype(jnp.bfloat16), grad_b.astype(jnp.bfloat16), grad_c.astype(jnp.bfloat16))


def solution(mesh):
    teach_n, seq_n = mesh.devices.shape
    n_y = FAM
    n_z = teach_n // n_y
    assert n_z == seq_n
    split = Mesh(mesh.devices.reshape(n_z, n_y, seq_n), ("tz", "ty", "seq"))
    placed = (
        P(TEACH, None, "seq"),
        P(TEACH, "seq", None),
        P(),
        P("seq", None, TEACH, None),
        P("seq", None, TEACH, None),
        P("seq", None, TEACH, None),
        P("seq", None, TEACH),
        P("seq", None),
        P(TEACH),
        P(TEACH),
    )
    return jax.shard_map(
        per_device,
        mesh=split,
        in_specs=placed,
        out_specs=(
            P("seq", None, TEACH, None),
            P("seq", None, TEACH, None),
            P("seq", None, TEACH, None),
        ),
        check_vma=False,
    )
```

```python
import jax
import jax.numpy as jnp
from jax import lax
from jax.sharding import Mesh
from jax.sharding import PartitionSpec as P

TD = 5120
P_SIZE = 64
FAM = 8
CAP = 32


EPS = 1e-06
HIGH = lax.Precision.HIGHEST
QUADRATIC = lax.Precision.HIGH
TEACH = ("tz", "ty")


def family_slots(fam_block):
    onehot = (fam_block[..., None] == jnp.arange(FAM, dtype=jnp.int32)[None, None, :]).astype(
        jnp.int32
    )
    before = jnp.cumsum(onehot, axis=1) - onehot
    return jnp.sum(before * onehot, axis=2)


def decay_matrix(log_sums, counts):
    places = jnp.arange(log_sums.shape[0])
    lower = places[:, None] >= places[None, :]
    same_doc = counts.T[:, :, None] == counts.T[:, None, :]
    keep_mask = (lower[None] & same_doc)[:, None]
    sums = log_sums.transpose(1, 2, 0)
    gaps = sums[:, :, :, None] - sums[:, :, None, :]
    return jnp.where(keep_mask, jnp.exp(jnp.where(keep_mask, gaps, 0.0)), 0.0)


def chain_weights(through_all, place, backward):
    count = through_all.shape[0]
    blocks = jnp.arange(count)
    s2 = blocks[:, None]
    s3 = blocks[None, :]
    if backward:
        used = (s3 > place) & (s3 < s2)
        live = blocks > place
    else:
        used = (s3 > s2) & (s3 < place)
        live = blocks < place
    factors = jnp.where(used[:, :, None, None], through_all[None], 1.0)
    weights = jnp.prod(factors, axis=1)
    return jnp.where(live[:, None, None], weights, 0.0)


def combine(weights, local_all):
    return jnp.sum(weights[:, :, :, None, None] * local_all.astype(jnp.float32), axis=0)


def ring_gather(x, axis):
    count = lax.axis_size(axis)
    ahead = [(i, (i + 1) % count) for i in range(count)]
    behind = [(i, (i - 1) % count) for i in range(count)]
    later = [None] * count
    later[0] = x
    cw = x
    ccw = x
    for hop in range(1, count // 2 + 1):
        cw = lax.ppermute(cw, axis, ahead)
        later[count - hop] = cw
        if hop < count - hop:
            ccw = lax.ppermute(ccw, axis, behind)
            later[hop] = ccw
    rel = jnp.stack(later)
    place = lax.axis_index(axis)
    doubled = jnp.concatenate([rel, rel])
    return lax.dynamic_slice_in_dim(doubled, (count - place) % count, count)


def per_device(
    teacher_in, teacher_proj, family, x_in, b_in, c_in, step_size, doc_start, a_rate, skip_gain
):
    n_z = lax.axis_size("tz")
    n_y = lax.axis_size("ty")
    seq_n = lax.axis_size("seq")
    teach_n = n_z * n_y
    heads_all = teach_n * x_in.shape[2]
    block_pos = teacher_in.shape[0]
    batch_n = teacher_in.shape[1]
    feat_width = teacher_in.shape[2]
    block_rows = block_pos * batch_n
    source = lax.axis_index("tz") * n_y + lax.axis_index("ty")

    own_fam = lax.dynamic_slice_in_dim(family, source * block_pos, block_pos).reshape(block_rows)
    slot_ids = family_slots(own_fam.reshape(1, block_rows))[0]
    dest_cols = own_fam * CAP + slot_ids
    select = (dest_cols[:, None] == jnp.arange(FAM * CAP, dtype=jnp.int32)[None, :]).astype(
        jnp.bfloat16
    )
    packed = jnp.einsum(
        "pbs,pbk->sk",
        select.reshape(block_pos, batch_n, FAM * CAP),
        teacher_in,
        preferred_element_type=jnp.float32,
    ).astype(jnp.bfloat16)
    packed = packed.reshape(FAM, CAP, feat_width)
    by_family = lax.all_to_all(packed, "ty", split_axis=0, concat_axis=0, tiled=True)
    received = ring_gather(by_family, "tz")
    x_full = x_in.astype(jnp.float32)
    b_full = b_in.astype(jnp.float32)
    c_full = c_in.astype(jnp.float32)
    log_sums = jnp.cumsum(-step_size * a_rate[None, None, :], axis=0)
    counts = jnp.cumsum(doc_start, axis=0)
    same_end = (counts == counts[-1][None, :]).astype(jnp.float32)
    to_end = jnp.exp(log_sums[-1][None] - log_sums) * same_end[:, :, None]
    from_start = jnp.exp(log_sums) * (counts == 0).astype(jnp.float32)[:, :, None]
    through = jnp.exp(log_sums[-1]) * (counts[-1] == 0).astype(jnp.float32)[:, None]
    inputs = step_size[..., None] * x_full
    local_state = jnp.einsum("jbh,jbhp,jbhn->bhpn", to_end, inputs, b_full, precision=HIGH)
    place = lax.axis_index("seq")
    through_hi = through.astype(jnp.bfloat16)
    through_lo = (through - through_hi.astype(jnp.float32)).astype(jnp.bfloat16)
    edge = local_state.shape[-1]
    packed_state = jnp.concatenate(
        [
            local_state.astype(jnp.bfloat16),
            jnp.broadcast_to(through_hi[:, :, None, None], through.shape + (1, edge)),
            jnp.broadcast_to(through_lo[:, :, None, None], through.shape + (1, edge)),
        ],
        axis=2,
    )
    slots_all = n_z * n_y * CAP
    received = received.reshape(slots_all, feat_width)
    weights = teacher_proj[0]
    partial_value = jnp.dot(received, weights, preferred_element_type=jnp.float32)
    sq_sums = jnp.sum(jnp.square(received.astype(jnp.float32)), axis=1)
    width = partial_value.shape[-1]
    group = n_y * CAP
    partial_value = partial_value.reshape(n_z, group, width)
    sq_all = sq_sums.reshape(n_z, group)
    sq_hi = sq_all.astype(jnp.bfloat16)
    sq_lo = (sq_all - sq_hi.astype(jnp.float32)).astype(jnp.bfloat16)
    sq_row = jnp.concatenate([sq_hi, sq_lo], axis=1)[:, None, :]
    state_rows = jnp.broadcast_to(
        packed_state.reshape(1, -1, width), (n_z, packed_state.size // width, width)
    )
    outbound = jnp.concatenate([partial_value.astype(jnp.bfloat16), sq_row, state_rows], axis=1)
    inbound = lax.all_to_all(outbound, "seq", split_axis=0, concat_axis=0, tiled=True)
    summed = jnp.sum(inbound[:, : group + 1].astype(jnp.float32), axis=0)
    gathered = inbound[:, group + 1 :].reshape((seq_n,) + packed_state.shape)
    rows = local_state.shape[2]
    through_all = gathered[:, :, :, rows, 0].astype(jnp.float32) + gathered[
        :, :, :, rows + 1, 0
    ].astype(jnp.float32)
    sq_total = summed[group, :group] + summed[group, group : 2 * group]
    row_scale = lax.rsqrt(sq_total / TD + EPS)
    scaled = (summed[:group] * row_scale[:, None]).astype(jnp.bfloat16)
    scaled = scaled.reshape(group, heads_all, -1)
    cols = scaled.shape[-1]
    outgoing = scaled.transpose(1, 2, 0)
    arrived = lax.all_to_all(outgoing, TEACH, split_axis=0, concat_axis=0, tiled=True)
    table = arrived.reshape(n_z, n_y, cols, n_y * CAP)

    shard_rows = n_y * block_rows
    shard_fam = lax.dynamic_slice_in_dim(
        family, lax.axis_index("seq") * (n_y * block_pos), n_y * block_pos
    ).reshape(n_y, block_rows)
    shard_slots = family_slots(shard_fam)
    sources = jnp.arange(n_y, dtype=jnp.int32)[:, None]
    row_index = ((shard_fam * n_y + sources) * CAP + shard_slots).reshape(shard_rows)
    chooser = (row_index[:, None] == jnp.arange(n_y * n_y * CAP, dtype=jnp.int32)[None, :]).astype(
        jnp.bfloat16
    )
    chooser = chooser.reshape(shard_rows, n_y, n_y * CAP)
    picked = jnp.einsum("rfq,jfcq->rjc", chooser, table, preferred_element_type=jnp.float32)
    target = picked.reshape(n_y * block_pos, batch_n, 1, P_SIZE)

    state_in = combine(chain_weights(through_all, place, False), gathered[:, :, :, :rows])
    decay_mat = decay_matrix(log_sums, counts)
    scores = jnp.einsum("ibhn,jbhn->bhij", c_in, b_in, preferred_element_type=jnp.float32)
    mixing = decay_mat * scores
    output = jnp.einsum("bhij,jbhp->ibhp", mixing, inputs, precision=QUADRATIC)
    output = output + from_start[..., None] * jnp.einsum(
        "ibhn,bhpn->ibhp", c_full, state_in, precision=HIGH
    )
    output = output + skip_gain[None, None, :, None] * x_full
    residual = output - target.astype(jnp.float32)
    local_adjoint = jnp.einsum("ibh,ibhn,ibhp->bhnp", from_start, c_full, residual, precision=HIGH)
    adjoint_all = lax.all_to_all(
        jnp.broadcast_to(local_adjoint.astype(jnp.bfloat16)[None], (seq_n,) + local_adjoint.shape),
        "seq",
        split_axis=0,
        concat_axis=0,
        tiled=True,
    )
    adjoint_in = combine(chain_weights(through_all, place, True), adjoint_all)
    grad_u = jnp.einsum("bhij,ibhp->jbhp", mixing, residual, precision=QUADRATIC)
    grad_u = grad_u + to_end[..., None] * jnp.einsum(
        "jbhn,bhnp->jbhp", b_full, adjoint_in, precision=HIGH
    )
    grad_x = step_size[..., None] * grad_u + skip_gain[None, None, :, None] * residual
    pair = decay_mat * jnp.einsum("ibhp,jbhp->bhij", residual, inputs, precision=QUADRATIC)
    grad_b = jnp.einsum("bhij,ibhn->jbhn", pair, c_full, precision=QUADRATIC)
    grad_b = grad_b + to_end[..., None] * jnp.einsum(
        "jbhp,bhnp->jbhn", inputs, adjoint_in, precision=HIGH
    )
    grad_c = jnp.einsum("bhij,jbhn->ibhn", pair, b_full, precision=QUADRATIC)
    grad_c = grad_c + from_start[..., None] * jnp.einsum(
        "ibhp,bhpn->ibhn", residual, state_in, precision=HIGH
    )
    return (grad_x.astype(jnp.bfloat16), grad_b.astype(jnp.bfloat16), grad_c.astype(jnp.bfloat16))


def solution(mesh):
    teach_n, seq_n = mesh.devices.shape
    n_y = FAM
    n_z = teach_n // n_y
    assert n_z == seq_n
    split = Mesh(mesh.devices.reshape(n_z, n_y, seq_n), ("tz", "ty", "seq"))
    placed = (
        P(TEACH, None, "seq"),
        P(TEACH, "seq", None),
        P(),
        P("seq", None, TEACH, None),
        P("seq", None, TEACH, None),
        P("seq", None, TEACH, None),
        P("seq", None, TEACH),
        P("seq", None),
        P(TEACH),
        P(TEACH),
    )
    return jax.shard_map(
        per_device,
        mesh=split,
        in_specs=placed,
        out_specs=(
            P("seq", None, TEACH, None),
            P("seq", None, TEACH, None),
            P("seq", None, TEACH, None),
        ),
        check_vma=False,
    )
```

```python
import jax
import jax.numpy as jnp
from jax import lax
from jax.sharding import Mesh
from jax.sharding import PartitionSpec as P

TD = 5120
P_SIZE = 64
FAM = 8
CAP = 32


EPS = 1e-06
HIGH = lax.Precision.HIGHEST
QUADRATIC = lax.Precision.HIGH
TEACH = ("tz", "ty")


def family_slots(fam_block):
    onehot = (fam_block[..., None] == jnp.arange(FAM, dtype=jnp.int32)[None, None, :]).astype(
        jnp.int32
    )
    before = jnp.cumsum(onehot, axis=1) - onehot
    return jnp.sum(before * onehot, axis=2)


def decay_matrix(log_sums, counts):
    places = jnp.arange(log_sums.shape[0])
    lower = places[:, None] >= places[None, :]
    same_doc = counts.T[:, :, None] == counts.T[:, None, :]
    keep_mask = (lower[None] & same_doc)[:, None]
    sums = log_sums.transpose(1, 2, 0)
    gaps = sums[:, :, :, None] - sums[:, :, None, :]
    return jnp.where(keep_mask, jnp.exp(jnp.where(keep_mask, gaps, 0.0)), 0.0)


def chain_weights(through_all, place, backward):
    count = through_all.shape[0]
    blocks = jnp.arange(count)
    s2 = blocks[:, None]
    s3 = blocks[None, :]
    if backward:
        used = (s3 > place) & (s3 < s2)
        live = blocks > place
    else:
        used = (s3 > s2) & (s3 < place)
        live = blocks < place
    factors = jnp.where(used[:, :, None, None], through_all[None], 1.0)
    weights = jnp.prod(factors, axis=1)
    return jnp.where(live[:, None, None], weights, 0.0)


def combine(weights, local_all):
    return jnp.sum(weights[:, :, :, None, None] * local_all.astype(jnp.float32), axis=0)


def ring_apply(x, axis, work):
    count = lax.axis_size(axis)
    ahead = [(i, (i + 1) % count) for i in range(count)]
    behind = [(i, (i - 1) % count) for i in range(count)]
    later = [None] * count
    later[0] = work(x)
    cw = x
    ccw = x
    for hop in range(1, count // 2 + 1):
        cw = lax.ppermute(cw, axis, ahead)
        later[count - hop] = work(cw)
        if hop < count - hop:
            ccw = lax.ppermute(ccw, axis, behind)
            later[hop] = work(ccw)
    place = lax.axis_index(axis)

    def order(*parts):
        rel = jnp.stack(parts)
        doubled = jnp.concatenate([rel, rel])
        return lax.dynamic_slice_in_dim(doubled, (count - place) % count, count)

    return jax.tree.map(order, *later)


def per_device(
    teacher_in, teacher_proj, family, x_in, b_in, c_in, step_size, doc_start, a_rate, skip_gain
):
    n_z = lax.axis_size("tz")
    n_y = lax.axis_size("ty")
    seq_n = lax.axis_size("seq")
    teach_n = n_z * n_y
    heads_all = teach_n * x_in.shape[2]
    block_pos = teacher_in.shape[0]
    batch_n = teacher_in.shape[1]
    feat_width = teacher_in.shape[2]
    block_rows = block_pos * batch_n
    source = lax.axis_index("tz") * n_y + lax.axis_index("ty")

    own_rows = teacher_in.reshape(block_rows, feat_width)
    own_fam = lax.dynamic_slice_in_dim(family, source * block_pos, block_pos).reshape(block_rows)
    slot_ids = family_slots(own_fam.reshape(1, block_rows))[0]
    dest_cols = own_fam * CAP + slot_ids
    select = (dest_cols[:, None] == jnp.arange(FAM * CAP, dtype=jnp.int32)[None, :]).astype(
        jnp.bfloat16
    )
    packed = jnp.dot(select.T, own_rows, preferred_element_type=jnp.float32).astype(jnp.bfloat16)
    packed = packed.reshape(FAM, CAP, feat_width)
    by_family = lax.all_to_all(packed, "ty", split_axis=0, concat_axis=0, tiled=True)
    x_full = x_in.astype(jnp.float32)
    b_full = b_in.astype(jnp.float32)
    c_full = c_in.astype(jnp.float32)
    log_sums = jnp.cumsum(-step_size * a_rate[None, None, :], axis=0)
    counts = jnp.cumsum(doc_start, axis=0)
    same_end = (counts == counts[-1][None, :]).astype(jnp.float32)
    to_end = jnp.exp(log_sums[-1][None] - log_sums) * same_end[:, :, None]
    from_start = jnp.exp(log_sums) * (counts == 0).astype(jnp.float32)[:, :, None]
    through = jnp.exp(log_sums[-1]) * (counts[-1] == 0).astype(jnp.float32)[:, None]
    inputs = step_size[..., None] * x_full
    local_state = jnp.einsum("jbh,jbhp,jbhn->bhpn", to_end, inputs, b_full, precision=HIGH)
    place = lax.axis_index("seq")
    through_hi = through.astype(jnp.bfloat16)
    through_lo = (through - through_hi.astype(jnp.float32)).astype(jnp.bfloat16)
    edge = local_state.shape[-1]
    packed_state = jnp.concatenate(
        [
            local_state.astype(jnp.bfloat16),
            jnp.broadcast_to(through_hi[:, :, None, None], through.shape + (1, edge)),
            jnp.broadcast_to(through_lo[:, :, None, None], through.shape + (1, edge)),
        ],
        axis=2,
    )
    weights = teacher_proj[0]

    def project(block):
        rows_in = block.reshape(-1, feat_width)
        value = jnp.dot(rows_in, weights, preferred_element_type=jnp.float32).astype(jnp.bfloat16)
        return value, jnp.sum(jnp.square(rows_in.astype(jnp.float32)), axis=1)

    partial_value, sq_sums = ring_apply(by_family, "tz", project)
    width = partial_value.shape[-1]
    group = n_y * CAP
    partial_value = partial_value.reshape(n_z, group, width)
    sq_all = sq_sums.reshape(n_z, group)
    sq_hi = sq_all.astype(jnp.bfloat16)
    sq_lo = (sq_all - sq_hi.astype(jnp.float32)).astype(jnp.bfloat16)
    sq_row = jnp.concatenate([sq_hi, sq_lo], axis=1)[:, None, :]
    state_rows = jnp.broadcast_to(
        packed_state.reshape(1, -1, width), (n_z, packed_state.size // width, width)
    )
    outbound = jnp.concatenate([partial_value, sq_row, state_rows], axis=1)
    inbound = lax.all_to_all(outbound, "seq", split_axis=0, concat_axis=0, tiled=True)
    summed = jnp.sum(inbound[:, : group + 1].astype(jnp.float32), axis=0)
    gathered = inbound[:, group + 1 :].reshape((seq_n,) + packed_state.shape)
    rows = local_state.shape[2]
    through_all = gathered[:, :, :, rows, 0].astype(jnp.float32) + gathered[
        :, :, :, rows + 1, 0
    ].astype(jnp.float32)
    sq_total = summed[group, :group] + summed[group, group : 2 * group]
    row_scale = lax.rsqrt(sq_total / TD + EPS)
    scaled = (summed[:group] * row_scale[:, None]).astype(jnp.bfloat16)
    scaled = scaled.reshape(group, heads_all, -1)
    cols = scaled.shape[-1]
    outgoing = scaled.transpose(1, 2, 0)
    arrived = lax.all_to_all(outgoing, TEACH, split_axis=0, concat_axis=0, tiled=True)
    table = arrived.reshape(n_z, n_y, cols, n_y * CAP)

    shard_rows = n_y * block_rows
    shard_fam = lax.dynamic_slice_in_dim(
        family, lax.axis_index("seq") * (n_y * block_pos), n_y * block_pos
    ).reshape(n_y, block_rows)
    shard_slots = family_slots(shard_fam)
    sources = jnp.arange(n_y, dtype=jnp.int32)[:, None]
    row_index = ((shard_fam * n_y + sources) * CAP + shard_slots).reshape(shard_rows)
    chooser = (row_index[:, None] == jnp.arange(n_y * n_y * CAP, dtype=jnp.int32)[None, :]).astype(
        jnp.bfloat16
    )
    chooser = chooser.reshape(shard_rows, n_y, n_y * CAP)
    picked = jnp.einsum("rfq,jfcq->rjc", chooser, table, preferred_element_type=jnp.float32)
    target = picked.reshape(n_y * block_pos, batch_n, 1, P_SIZE)

    state_in = combine(chain_weights(through_all, place, False), gathered[:, :, :, :rows])
    decay_mat = decay_matrix(log_sums, counts)
    scores = jnp.einsum("ibhn,jbhn->bhij", c_in, b_in, preferred_element_type=jnp.float32)
    mixing = decay_mat * scores
    output = jnp.einsum("bhij,jbhp->ibhp", mixing, inputs, precision=QUADRATIC)
    output = output + from_start[..., None] * jnp.einsum(
        "ibhn,bhpn->ibhp", c_full, state_in, precision=HIGH
    )
    output = output + skip_gain[None, None, :, None] * x_full
    residual = output - target.astype(jnp.float32)
    local_adjoint = jnp.einsum("ibh,ibhn,ibhp->bhnp", from_start, c_full, residual, precision=HIGH)
    adjoint_all = lax.all_to_all(
        jnp.broadcast_to(local_adjoint.astype(jnp.bfloat16)[None], (seq_n,) + local_adjoint.shape),
        "seq",
        split_axis=0,
        concat_axis=0,
        tiled=True,
    )
    adjoint_in = combine(chain_weights(through_all, place, True), adjoint_all)
    grad_u = jnp.einsum("bhij,ibhp->jbhp", mixing, residual, precision=QUADRATIC)
    grad_u = grad_u + to_end[..., None] * jnp.einsum(
        "jbhn,bhnp->jbhp", b_full, adjoint_in, precision=HIGH
    )
    grad_x = step_size[..., None] * grad_u + skip_gain[None, None, :, None] * residual
    pair = decay_mat * jnp.einsum("ibhp,jbhp->bhij", residual, inputs, precision=QUADRATIC)
    grad_b = jnp.einsum("bhij,ibhn->jbhn", pair, c_full, precision=QUADRATIC)
    grad_b = grad_b + to_end[..., None] * jnp.einsum(
        "jbhp,bhnp->jbhn", inputs, adjoint_in, precision=HIGH
    )
    grad_c = jnp.einsum("bhij,jbhn->ibhn", pair, b_full, precision=QUADRATIC)
    grad_c = grad_c + from_start[..., None] * jnp.einsum(
        "ibhp,bhpn->ibhn", residual, state_in, precision=HIGH
    )
    return (grad_x.astype(jnp.bfloat16), grad_b.astype(jnp.bfloat16), grad_c.astype(jnp.bfloat16))


def solution(mesh):
    teach_n, seq_n = mesh.devices.shape
    n_y = FAM
    n_z = teach_n // n_y
    assert n_z == seq_n
    split = Mesh(mesh.devices.reshape(n_z, n_y, seq_n), ("tz", "ty", "seq"))
    placed = (
        P(TEACH, None, "seq"),
        P(TEACH, "seq", None),
        P(),
        P("seq", None, TEACH, None),
        P("seq", None, TEACH, None),
        P("seq", None, TEACH, None),
        P("seq", None, TEACH),
        P("seq", None),
        P(TEACH),
        P(TEACH),
    )
    return jax.shard_map(
        per_device,
        mesh=split,
        in_specs=placed,
        out_specs=(
            P("seq", None, TEACH, None),
            P("seq", None, TEACH, None),
            P("seq", None, TEACH, None),
        ),
        check_vma=False,
    )
```
